128 devices in a mesh: grp: 8 (over z, core), dev: 16 (over y, x).
Axes of the slice: x: 4, y: 4, z: 4, core: 2. Of those that a mesh axis runs over, the one named last changes fastest.
Arguments:
- positions: float32 [3, 131072], P(None, ('grp', 'dev')), may hold values from -3 to 3
- velocities: float32 [3, 131072], P(None, ('grp', 'dev')), may hold values from -5 to 5
- accelerations: float32 [3, 131072], P(None, ('grp', 'dev')), may hold values from -3 to 3
- jerks: float32 [3, 131072], P(None, ('grp', 'dev')), may hold values from -3 to 3
- levels: int32 [131072], P(('grp', 'dev')), may hold values from 0 to 5
- counts: int32 [2, 128], replicated, may hold values from 1 to 256, 16384 in all within a row
- active_rows: int32 [2, 32768], P(None, ('grp', 'dev')), may hold values from 0 to 1023, as said below
Outputs:
- new_positions: float32 [3, 131072], P(None, ('grp', 'dev'))
- new_velocities: float32 [3, 131072], P(None, ('grp', 'dev'))
- new_accelerations: float32 [3, 131072], P(None, ('grp', 'dev'))
- new_jerks: float32 [3, 131072], P(None, ('grp', 'dev'))
The draws below stay inside these ranges and needn't reach their ends.
Inputs may be any that keep to these rules, and one draw needn't show every extreme that they name: In each step the 128 counts sum to exactly 16384 and the largest of them is exactly 256. `active_rows`: for each step and device, the 256 entries of the device's slots are distinct indices of that device's own stars; only the first counts of them are live.
All inputs are finite; a program needn't handle non-finite values.
Results may differ from the reference program's by a relative error of at most 0.00022.
Values sent between devices are 32-bit elements; how exact they have to be, the bound alone decides.
No kernel may reach another device: no remote copies, remote signals or barrier semaphores. Data moves between devices by JAX's collectives and lax.ppermute only.
A program may use at most 128 MiB of HBM per device.

```python
import math
import jax
import jax.numpy as jnp
import numpy as np
from jax import lax

STAR_DEV = 1024
ACT_CAP = 256
STEPS = 2
LEVELS = 6
STARS = 131072
ACTIVE = 16384
DEVICES = 128


def draw_active_rows(key, part):
    keys = jax.random.split(jax.random.fold_in(key, 7), STEPS * DEVICES)
    chosen = jax.vmap(lambda single: jax.random.permutation(single, STAR_DEV)[:ACT_CAP])(keys)
    return chosen.reshape(STEPS, DEVICES * ACT_CAP).astype(jnp.int32)


def place_ends(entries, key, low, top_value):
    dims = entries.shape
    spot = [jax.random.randint(jax.random.fold_in(key, axis), (), 0, dims[axis]) for axis in range(len(dims))]
    entries = entries.at[tuple(spot)].set(low)
    longest = dims.index(max(dims))
    spot[longest] = (spot[longest] + 1) % dims[longest]
    return entries.at[tuple(spot)].set(top_value)


def steps_of(stream_key, extent, cuts, low, top_value):
    loudness = 1.0
    for axis_at, shards_of in cuts:
        heights = jax.random.uniform(jax.random.fold_in(jax.random.fold_in(stream_key, 6), axis_at), (shards_of,), jnp.float32, low / len(cuts), top_value / len(cuts))
        loudness = loudness * jnp.repeat(jnp.exp(heights), extent[axis_at] // shards_of).reshape((-1,) + (1,) * (len(extent) - 1 - axis_at))
    return loudness


def length_profile(amount, total, limit, slope):
    portions = [(1 << 20) // math.isqrt(grade ** slope) + 1 for grade in range(2, amount + 1)]
    spare, given = total - limit - (amount - 1), [1] * (amount - 1)
    while spare > 0:
        candidates = [i for i in range(amount - 1) if given[i] < limit]
        whole, budget = sum([portions[i] for i in candidates]), spare
        for i in candidates:
            more = min(limit - given[i], max(1, budget * portions[i] // whole), spare)
            given[i] = given[i] + more
            spare = spare - more
    return np.array([limit] + given)


def uneven_parts(stream_key, count, total, most, lean):
    if count == 2:
        one = jax.random.randint(stream_key, (), max(1, total - most), min(most, total - 1) + 1)
        return jnp.stack([one, total - one])
    tallies = jnp.asarray(length_profile(count, total, most, lean), jnp.int32)
    couples = (count - 1) // 2
    source_of, taker = tallies[1:1 + 2 * couples:2], tallies[2:2 + 2 * couples:2]
    room = jnp.minimum(source_of - 1, most - taker)
    passed = jax.random.randint(jax.random.fold_in(stream_key, 1), (couples,), 0, 1 << 20) % (room + 1)
    tallies = tallies.at[1:1 + 2 * couples:2].set(source_of - passed).at[2:2 + 2 * couples:2].set(taker + passed)
    return tallies[jax.random.permutation(jax.random.fold_in(stream_key, 2), count)]


def scatter_about(key, dims, width, limit, shards=(), kind=jnp.bfloat16):
    result = width * jax.random.normal(key, dims, jnp.float32)
    if shards:
        result = result * steps_of(key, dims, shards, -0.22, 0.18)
    return jnp.clip(result, -limit, limit).astype(kind)


def setup_inputs(seed: int = 0) -> dict:
    splits = jax.random.split(jax.random.key(seed), 8)
    positions = scatter_about(splits[0], (3, STARS), 0.5, 3.0, ((1, 128),), jnp.float32)
    velocities = scatter_about(splits[1], (3, STARS), 1.0, 5.0, ((1, 128),), jnp.float32)
    accelerations = scatter_about(splits[2], (3, STARS), 0.5, 3.0, ((1, 128),), jnp.float32)
    jerks = scatter_about(splits[3], (3, STARS), 0.5, 3.0, ((1, 128),), jnp.float32)
    levels = place_ends(jax.random.randint(splits[4], (STARS,), 0, LEVELS), jax.random.fold_in(splits[4], 1), 0, LEVELS - 1).astype(jnp.int32)
    counts = jax.vmap(lambda own: uneven_parts(own, DEVICES, ACTIVE, ACT_CAP, 2))(jax.random.split(splits[5], STEPS)).reshape((STEPS, DEVICES)).astype(jnp.int32)
    active_rows = draw_active_rows(jax.random.fold_in(splits[7], 71), 0)
    return dict(positions=positions, velocities=velocities, accelerations=accelerations, jerks=jerks, levels=levels, counts=counts, active_rows=active_rows)


tick_length = 1.0 / 128.0

def pair_block(targets, src_pos, src_vel, mass, soft_sq):
    gap_x = src_pos[0][None, :] - targets[0][:, None]
    gap_y = src_pos[1][None, :] - targets[1][:, None]
    gap_z = src_pos[2][None, :] - targets[2][:, None]
    drift_x = src_vel[0][None, :] - targets[3][:, None]
    drift_y = src_vel[1][None, :] - targets[4][:, None]
    drift_z = src_vel[2][None, :] - targets[5][:, None]
    squared = gap_x * gap_x + gap_y * gap_y + gap_z * gap_z + soft_sq
    inverse = lax.rsqrt(squared)
    weight = mass * inverse * inverse * inverse
    along = 3.0 * (gap_x * drift_x + gap_y * drift_y + gap_z * drift_z) * inverse * inverse
    return jnp.stack([lax.optimization_barrier(jnp.sum(weight * gap_x, axis=1)), lax.optimization_barrier(jnp.sum(weight * gap_y, axis=1)), lax.optimization_barrier(jnp.sum(weight * gap_z, axis=1)), lax.optimization_barrier(jnp.sum(weight * (drift_x - along * gap_x), axis=1)), lax.optimization_barrier(jnp.sum(weight * (drift_y - along * gap_y), axis=1)), lax.optimization_barrier(jnp.sum(weight * (drift_z - along * gap_z), axis=1))])

def predict(positions, velocities, accelerations, jerks, elapsed):
    span = elapsed[None, :]
    pred_pos = positions + span * velocities + 0.5 * span * span * accelerations + span * span * span / 6.0 * jerks
    pred_vel = velocities + span * accelerations + 0.5 * span * span * jerks
    return (pred_pos, pred_vel)

def correct(old_pos, old_vel, old_acc, old_jerk, force, jerk_new, span):
    span = span[None, :]
    new_vel = old_vel + 0.5 * span * (old_acc + force) + span * span / 12.0 * (old_jerk - jerk_new)
    new_pos = old_pos + 0.5 * span * (old_vel + new_vel) + span * span / 12.0 * (old_acc - force)
    return (new_pos, new_vel)

def reference(positions, velocities, accelerations, jerks, levels, counts, active_rows):
    mass = 1.0 / STARS
    soft_sq = 0.0004 * (131072.0 / STARS) ** (2.0 / 3.0)
    last_time = -(jnp.left_shift(jnp.int32(1), levels) - 1).astype(jnp.float32) * tick_length
    for step in range(STEPS):
        now = (step + 1) * tick_length
        pred_pos, pred_vel = predict(positions, velocities, accelerations, jerks, now - last_time)
        step_counts = counts[step]
        inclusive = jnp.cumsum(step_counts).astype(jnp.int32)
        first = (inclusive - step_counts).astype(jnp.int32)
        place = jnp.arange(ACTIVE, dtype=jnp.int32)
        owner = lax.optimization_barrier(jnp.sum((inclusive[None, :] <= place[:, None]).astype(jnp.int32), axis=1)).astype(jnp.int32)
        slot = (owner * ACT_CAP + place - first[owner]).astype(jnp.int32)
        ident = (owner * STAR_DEV + active_rows[step][slot]).astype(jnp.int32)
        targets = jnp.concatenate([pred_pos[:, ident], pred_vel[:, ident]], axis=0)
        block = math.gcd(ACTIVE, 64)
        grouped = targets.reshape(6, ACTIVE // block, block).transpose(1, 0, 2)
        sums = lax.map(lambda part_rows: pair_block(part_rows, pred_pos, pred_vel, mass, soft_sq), grouped)
        sums = sums.transpose(1, 0, 2).reshape(6, ACTIVE)
        span = now - last_time[ident]
        new_pos, new_vel = correct(positions[:, ident], velocities[:, ident], accelerations[:, ident], jerks[:, ident], sums[:3], sums[3:], span)
        positions = positions.at[:, ident].set(new_pos)
        velocities = velocities.at[:, ident].set(new_vel)
        accelerations = accelerations.at[:, ident].set(sums[:3])
        jerks = jerks.at[:, ident].set(sums[3:])
        last_time = last_time.at[ident].set(now)
    return (positions, velocities, accelerations, jerks)
```

```python
import math

import jax
import jax.numpy as jnp
from jax import lax
from jax.sharding import PartitionSpec as P

tick_length = 1.0 / 128.0


def pair_block(targets, src_pos, src_vel, mass, soft_sq):
    gap_x = src_pos[0][None, :] - targets[0][:, None]
    gap_y = src_pos[1][None, :] - targets[1][:, None]
    gap_z = src_pos[2][None, :] - targets[2][:, None]
    drift_x = src_vel[0][None, :] - targets[3][:, None]
    drift_y = src_vel[1][None, :] - targets[4][:, None]
    drift_z = src_vel[2][None, :] - targets[5][:, None]
    squared = gap_x * gap_x + gap_y * gap_y + gap_z * gap_z + soft_sq
    inverse = lax.rsqrt(squared)
    weight = mass * inverse * inverse * inverse
    along = 3.0 * (gap_x * drift_x + gap_y * drift_y + gap_z * drift_z) * inverse * inverse
    return jnp.stack(
        [
            jnp.sum(weight * gap_x, axis=1),
            jnp.sum(weight * gap_y, axis=1),
            jnp.sum(weight * gap_z, axis=1),
            jnp.sum(weight * (drift_x - along * gap_x), axis=1),
            jnp.sum(weight * (drift_y - along * gap_y), axis=1),
            jnp.sum(weight * (drift_z - along * gap_z), axis=1),
        ]
    )


def block_terms(packed, src_pos, src_vel, mass, soft_sq):
    width, total = packed.shape
    block = math.gcd(total, 2048)
    grouped = packed.reshape(width, total // block, block).transpose(1, 0, 2)
    result = lax.map(lambda targets: pair_block(targets, src_pos, src_vel, mass, soft_sq), grouped)
    return result.transpose(1, 0, 2).reshape(width, total)


def predict(positions, velocities, accelerations, jerks, elapsed):
    span = elapsed[None, :]
    pred_pos = (
        positions
        + span * velocities
        + 0.5 * span * span * accelerations
        + span * span * span / 6.0 * jerks
    )
    pred_vel = velocities + span * accelerations + 0.5 * span * span * jerks
    return (pred_pos, pred_vel)


def correct(old_pos, old_vel, old_acc, old_jerk, force, jerk_new, span):
    span = span[None, :]
    new_vel = old_vel + 0.5 * span * (old_acc + force) + span * span / 12.0 * (old_jerk - jerk_new)
    new_pos = old_pos + 0.5 * span * (old_vel + new_vel) + span * span / 12.0 * (old_acc - force)
    return (new_pos, new_vel)


def shards(positions, velocities, accelerations, jerks, levels, counts, active_rows):
    devices_all = lax.axis_size("grp") * lax.axis_size("dev")
    my_rank = lax.axis_index("grp") * lax.axis_size("dev") + lax.axis_index("dev")
    star_dev = positions.shape[1]
    slot_cap = active_rows.shape[1]
    stars_all = star_dev * devices_all
    live_all = stars_all // 8
    mass = 1.0 / stars_all
    soft_sq = 0.0004 * (131072.0 / stars_all) ** (2.0 / 3.0)
    chunks = 4
    chunk = live_all // chunks
    last_time = -(jnp.left_shift(jnp.int32(1), levels) - 1).astype(jnp.float32) * tick_length
    for step in range(active_rows.shape[0]):
        now = (step + 1) * tick_length
        pred_pos, pred_vel = predict(positions, velocities, accelerations, jerks, now - last_time)
        rows = active_rows[step]
        targets = jnp.concatenate([pred_pos[:, rows], pred_vel[:, rows]], axis=0)
        step_counts = counts[step]
        own_count = step_counts[my_rank]
        inclusive = jnp.cumsum(step_counts).astype(jnp.int32)
        first = inclusive - step_counts
        place = jnp.arange(live_all, dtype=jnp.int32)
        owner = jnp.sum((inclusive[None, :] <= place[:, None]).astype(jnp.int32), axis=1)
        owner = jnp.minimum(owner, devices_all - 1)
        slot = owner * slot_cap + place - first[owner]
        gathered = lax.all_gather(targets[None], ("grp", "dev"), axis=0, tiled=True)
        flat = gathered.transpose(1, 0, 2).reshape(6, devices_all * slot_cap)
        compact = flat[:, slot]
        parts = []
        summed = None
        for c in range(chunks):
            piece = compact[:, c * chunk:(c + 1) * chunk]
            terms = block_terms(piece, pred_pos, pred_vel, mass, soft_sq)
            if summed is not None:
                terms, summed = lax.optimization_barrier((terms, summed))
                parts.append(summed)
            summed = lax.psum(terms, ("grp", "dev"))
        parts.append(summed)
        parts.append(jnp.zeros((6, slot_cap), jnp.float32))
        totals = jnp.concatenate(parts, axis=1)
        own = lax.dynamic_slice_in_dim(totals, first[my_rank], slot_cap, 1)
        span = now - last_time[rows]
        new_pos, new_vel = correct(
            positions[:, rows],
            velocities[:, rows],
            accelerations[:, rows],
            jerks[:, rows],
            own[:3],
            own[3:],
            span,
        )
        live = jnp.arange(slot_cap, dtype=jnp.int32) < own_count
        target = jnp.where(live, rows, star_dev)
        positions = positions.at[:, target].set(new_pos, mode="drop")
        velocities = velocities.at[:, target].set(new_vel, mode="drop")
        accelerations = accelerations.at[:, target].set(own[:3], mode="drop")
        jerks = jerks.at[:, target].set(own[3:], mode="drop")
        last_time = last_time.at[target].set(now, mode="drop")
    return (positions, velocities, accelerations, jerks)


def solution(mesh):
    placed = (
        P(None, ("grp", "dev")),
        P(None, ("grp", "dev")),
        P(None, ("grp", "dev")),
        P(None, ("grp", "dev")),
        P(("grp", "dev")),
        P(),
        P(None, ("grp", "dev")),
    )
    return jax.shard_map(
        shards,
        mesh=mesh,
        in_specs=placed,
        out_specs=(
            P(None, ("grp", "dev")),
            P(None, ("grp", "dev")),
            P(None, ("grp", "dev")),
            P(None, ("grp", "dev")),
        ),
        check_vma=False,
    )
```

```python
import math

import jax
import jax.numpy as jnp
from jax import lax
from jax.sharding import PartitionSpec as P

tick_length = 1.0 / 128.0


def pair_block(targets, src_pos, src_vel, mass, soft_sq):
    gap_x = src_pos[0][None, :] - targets[0][:, None]
    gap_y = src_pos[1][None, :] - targets[1][:, None]
    gap_z = src_pos[2][None, :] - targets[2][:, None]
    drift_x = src_vel[0][None, :] - targets[3][:, None]
    drift_y = src_vel[1][None, :] - targets[4][:, None]
    drift_z = src_vel[2][None, :] - targets[5][:, None]
    squared = gap_x * gap_x + gap_y * gap_y + gap_z * gap_z + soft_sq
    inverse = lax.rsqrt(squared)
    weight = mass * inverse * inverse * inverse
    along = 3.0 * (gap_x * drift_x + gap_y * drift_y + gap_z * drift_z) * inverse * inverse
    return jnp.stack(
        [
            jnp.sum(weight * gap_x, axis=1),
            jnp.sum(weight * gap_y, axis=1),
            jnp.sum(weight * gap_z, axis=1),
            jnp.sum(weight * (drift_x - along * gap_x), axis=1),
            jnp.sum(weight * (drift_y - along * gap_y), axis=1),
            jnp.sum(weight * (drift_z - along * gap_z), axis=1),
        ]
    )


def block_terms(packed, src_pos, src_vel, mass, soft_sq):
    width, total = packed.shape
    block = math.gcd(total, 2048)
    grouped = packed.reshape(width, total // block, block).transpose(1, 0, 2)
    result = lax.map(lambda targets: pair_block(targets, src_pos, src_vel, mass, soft_sq), grouped)
    return result.transpose(1, 0, 2).reshape(width, total)


def predict(positions, velocities, accelerations, jerks, elapsed):
    span = elapsed[None, :]
    pred_pos = (
        positions
        + span * velocities
        + 0.5 * span * span * accelerations
        + span * span * span / 6.0 * jerks
    )
    pred_vel = velocities + span * accelerations + 0.5 * span * span * jerks
    return (pred_pos, pred_vel)


def correct(old_pos, old_vel, old_acc, old_jerk, force, jerk_new, span):
    span = span[None, :]
    new_vel = old_vel + 0.5 * span * (old_acc + force) + span * span / 12.0 * (old_jerk - jerk_new)
    new_pos = old_pos + 0.5 * span * (old_vel + new_vel) + span * span / 12.0 * (old_acc - force)
    return (new_pos, new_vel)


def shards(positions, velocities, accelerations, jerks, levels, counts, active_rows):
    n_grp = lax.axis_size("grp")
    n_dev = lax.axis_size("dev")
    g_idx = lax.axis_index("grp")
    d_idx = lax.axis_index("dev")
    devices_all = n_grp * n_dev
    star_dev = positions.shape[1]
    slot_cap = active_rows.shape[1]
    stars_all = star_dev * devices_all
    mass = 1.0 / stars_all
    soft_sq = 0.0004 * (131072.0 / stars_all) ** (2.0 / 3.0)
    col_cap = n_grp * slot_cap
    block = 256
    last_time = -(jnp.left_shift(jnp.int32(1), levels) - 1).astype(jnp.float32) * tick_length
    for step in range(active_rows.shape[0]):
        now = (step + 1) * tick_length
        pred_pos, pred_vel = predict(positions, velocities, accelerations, jerks, now - last_time)
        rows = active_rows[step]
        targets = jnp.concatenate([pred_pos[:, rows], pred_vel[:, rows]], axis=0)
        col_counts = counts[step].reshape(n_grp, n_dev)[:, d_idx]
        inclusive = jnp.cumsum(col_counts).astype(jnp.int32)
        first = inclusive - col_counts
        col_live = inclusive[-1]
        place = jnp.arange(col_cap, dtype=jnp.int32)
        owner = jnp.sum((inclusive[None, :] <= place[:, None]).astype(jnp.int32), axis=1)
        owner = jnp.minimum(owner, n_grp - 1)
        slot = jnp.clip(owner * slot_cap + place - first[owner], 0, col_cap - 1)
        col_targets = lax.all_gather(targets, "grp", axis=1, tiled=True)
        compact = col_targets[:, slot]
        src = lax.all_gather(jnp.concatenate([pred_pos, pred_vel], axis=0), "dev", axis=1, tiled=True)
        n_blocks = (col_live + block - 1) // block

        def body(b, acc):
            piece = lax.dynamic_slice_in_dim(compact, b * block, block, 1)
            terms = pair_block(piece, src[:3], src[3:], mass, soft_sq)
            return lax.dynamic_update_slice_in_dim(acc, terms, b * block, 1)

        partial = lax.fori_loop(0, n_blocks, body, jnp.zeros((6, col_cap), jnp.float32))
        totals = lax.psum(partial, "grp")
        totals = jnp.concatenate([totals, jnp.zeros((6, slot_cap), jnp.float32)], axis=1)
        own = lax.dynamic_slice_in_dim(totals, first[g_idx], slot_cap, 1)
        own_count = col_counts[g_idx]
        span = now - last_time[rows]
        new_pos, new_vel = correct(
            positions[:, rows],
            velocities[:, rows],
            accelerations[:, rows],
            jerks[:, rows],
            own[:3],
            own[3:],
            span,
        )
        live = jnp.arange(slot_cap, dtype=jnp.int32) < own_count
        target = jnp.where(live, rows, star_dev)
        positions = positions.at[:, target].set(new_pos, mode="drop")
        velocities = velocities.at[:, target].set(new_vel, mode="drop")
        accelerations = accelerations.at[:, target].set(own[:3], mode="drop")
        jerks = jerks.at[:, target].set(own[3:], mode="drop")
        last_time = last_time.at[target].set(now, mode="drop")
    return (positions, velocities, accelerations, jerks)


def solution(mesh):
    placed = (
        P(None, ("grp", "dev")),
        P(None, ("grp", "dev")),
        P(None, ("grp", "dev")),
        P(None, ("grp", "dev")),
        P(("grp", "dev")),
        P(),
        P(None, ("grp", "dev")),
    )
    return jax.shard_map(
        shards,
        mesh=mesh,
        in_specs=placed,
        out_specs=(
            P(None, ("grp", "dev")),
            P(None, ("grp", "dev")),
            P(None, ("grp", "dev")),
            P(None, ("grp", "dev")),
        ),
        check_vma=False,
    )
```

```python
import math

import jax
import jax.numpy as jnp
from jax import lax
from jax.experimental import pallas as pl
from jax.experimental.pallas import tpu as pltpu
from jax.sharding import PartitionSpec as P

tick_length = 1.0 / 128.0


LANES = 128
SUB = 8


def _pair_terms_kernel(n_ref, tgt_ref, src_ref, out_ref, *, soft_sq, mass, n_chunks):
    out_ref[...] = jnp.zeros(out_ref.shape, jnp.float32)

    def one_group(gi, carry):
        base = pl.multiple_of(gi * (2 * SUB), 2 * SUB)
        tile = tgt_ref[pl.ds(base, 2 * SUB), :]
        halves = []
        for h in range(2):
            part = tile[h * SUB:(h + 1) * SUB, :]
            halves.append([jnp.broadcast_to(part[:, k:k + 1], (SUB, LANES)) for k in range(6)])

        def chunk(c, accs):
            off = pl.multiple_of(c * LANES, LANES)
            s = [src_ref[k, :, pl.ds(off, LANES)] for k in range(6)]
            new = []
            for h in range(2):
                t = halves[h]
                a = accs[6 * h:6 * h + 6]
                dx = s[0] - t[0]
                dy = s[1] - t[1]
                dz = s[2] - t[2]
                ux = s[3] - t[3]
                uy = s[4] - t[4]
                uz = s[5] - t[5]
                r2 = dx * dx + dy * dy + dz * dz + soft_sq
                inv = lax.rsqrt(r2)
                inv2 = inv * inv
                w = inv * inv2
                al = 3.0 * (dx * ux + dy * uy + dz * uz) * inv2
                new += [
                    a[0] + w * dx,
                    a[1] + w * dy,
                    a[2] + w * dz,
                    a[3] + w * (ux - al * dx),
                    a[4] + w * (uy - al * dy),
                    a[5] + w * (uz - al * dz),
                ]
            return tuple(new)

        zero = jnp.zeros((SUB, LANES), jnp.float32)
        accs = lax.fori_loop(0, n_chunks, chunk, (zero,) * 12, unroll=2)
        for h in range(2):
            for k in range(6):
                total = jnp.sum(accs[6 * h + k], axis=1, keepdims=True) * mass
                out_ref[pl.ds(base + h * SUB, SUB), pl.ds(k, 1)] = total
        return carry

    lax.fori_loop(0, n_ref[0], one_group, 0)


def pair_terms(n_groups, tgt, src, mass, soft_sq, interpret=False):
    cap = tgt.shape[0]
    n_src = src.shape[1]
    src_b = jnp.broadcast_to(src[:, None, :], (6, SUB, n_src))
    kernel = lambda *refs: _pair_terms_kernel(*refs, soft_sq=soft_sq, mass=mass, n_chunks=n_src // LANES)
    return pl.pallas_call(
        kernel,
        out_shape=jax.ShapeDtypeStruct((cap, 8), jnp.float32),
        in_specs=[
            pl.BlockSpec(memory_space=pltpu.SMEM),
            pl.BlockSpec(memory_space=pltpu.VMEM),
            pl.BlockSpec(memory_space=pltpu.VMEM),
        ],
        out_specs=pl.BlockSpec(memory_space=pltpu.VMEM),
        interpret=interpret,
    )(jnp.reshape(n_groups, (1,)).astype(jnp.int32), tgt, src_b)


def pair_block(targets, src_pos, src_vel, mass, soft_sq):
    gap_x = src_pos[0][None, :] - targets[0][:, None]
    gap_y = src_pos[1][None, :] - targets[1][:, None]
    gap_z = src_pos[2][None, :] - targets[2][:, None]
    drift_x = src_vel[0][None, :] - targets[3][:, None]
    drift_y = src_vel[1][None, :] - targets[4][:, None]
    drift_z = src_vel[2][None, :] - targets[5][:, None]
    squared = gap_x * gap_x + gap_y * gap_y + gap_z * gap_z + soft_sq
    inverse = lax.rsqrt(squared)
    weight = mass * inverse * inverse * inverse
    along = 3.0 * (gap_x * drift_x + gap_y * drift_y + gap_z * drift_z) * inverse * inverse
    return jnp.stack(
        [
            jnp.sum(weight * gap_x, axis=1),
            jnp.sum(weight * gap_y, axis=1),
            jnp.sum(weight * gap_z, axis=1),
            jnp.sum(weight * (drift_x - along * gap_x), axis=1),
            jnp.sum(weight * (drift_y - along * gap_y), axis=1),
            jnp.sum(weight * (drift_z - along * gap_z), axis=1),
        ]
    )


def block_terms(packed, src_pos, src_vel, mass, soft_sq):
    width, total = packed.shape
    block = math.gcd(total, 2048)
    grouped = packed.reshape(width, total // block, block).transpose(1, 0, 2)
    result = lax.map(lambda targets: pair_block(targets, src_pos, src_vel, mass, soft_sq), grouped)
    return result.transpose(1, 0, 2).reshape(width, total)


def predict(positions, velocities, accelerations, jerks, elapsed):
    span = elapsed[None, :]
    pred_pos = (
        positions
        + span * velocities
        + 0.5 * span * span * accelerations
        + span * span * span / 6.0 * jerks
    )
    pred_vel = velocities + span * accelerations + 0.5 * span * span * jerks
    return (pred_pos, pred_vel)


def correct(old_pos, old_vel, old_acc, old_jerk, force, jerk_new, span):
    span = span[None, :]
    new_vel = old_vel + 0.5 * span * (old_acc + force) + span * span / 12.0 * (old_jerk - jerk_new)
    new_pos = old_pos + 0.5 * span * (old_vel + new_vel) + span * span / 12.0 * (old_acc - force)
    return (new_pos, new_vel)


def shards(positions, velocities, accelerations, jerks, levels, counts, active_rows):
    n_grp = lax.axis_size("grp")
    n_dev = lax.axis_size("dev")
    g_idx = lax.axis_index("grp")
    d_idx = lax.axis_index("dev")
    devices_all = n_grp * n_dev
    star_dev = positions.shape[1]
    slot_cap = active_rows.shape[1]
    stars_all = star_dev * devices_all
    mass = 1.0 / stars_all
    soft_sq = 0.0004 * (131072.0 / stars_all) ** (2.0 / 3.0)
    col_cap = n_grp * slot_cap
    last_time = -(jnp.left_shift(jnp.int32(1), levels) - 1).astype(jnp.float32) * tick_length
    for step in range(active_rows.shape[0]):
        now = (step + 1) * tick_length
        pred_pos, pred_vel = predict(positions, velocities, accelerations, jerks, now - last_time)
        rows = active_rows[step]
        targets = jnp.concatenate([pred_pos[:, rows], pred_vel[:, rows]], axis=0)
        col_counts = counts[step].reshape(n_grp, n_dev)[:, d_idx]
        inclusive = jnp.cumsum(col_counts).astype(jnp.int32)
        first = inclusive - col_counts
        col_live = inclusive[-1]
        place = jnp.arange(col_cap, dtype=jnp.int32)
        owner = jnp.sum((inclusive[None, :] <= place[:, None]).astype(jnp.int32), axis=1)
        owner = jnp.minimum(owner, n_grp - 1)
        slot = jnp.clip(owner * slot_cap + place - first[owner], 0, col_cap - 1)
        col_targets = lax.all_gather(targets, "grp", axis=1, tiled=True)
        padded = jnp.concatenate([col_targets, jnp.zeros((2, col_cap), jnp.float32)], axis=0)
        compact = padded.T[slot]
        src = lax.all_gather(jnp.concatenate([pred_pos, pred_vel], axis=0), "dev", axis=1, tiled=True)
        n_groups = (col_live + 2 * SUB - 1) // (2 * SUB)
        partial = pair_terms(n_groups, compact, src, mass, soft_sq)
        totals = lax.psum(partial, "grp")
        totals = jnp.concatenate([totals, jnp.zeros((slot_cap, 8), jnp.float32)], axis=0)
        own = lax.dynamic_slice_in_dim(totals, first[g_idx], slot_cap, 0)[:, :6].T
        own_count = col_counts[g_idx]
        span = now - last_time[rows]
        new_pos, new_vel = correct(
            positions[:, rows],
            velocities[:, rows],
            accelerations[:, rows],
            jerks[:, rows],
            own[:3],
            own[3:],
            span,
        )
        live = jnp.arange(slot_cap, dtype=jnp.int32) < own_count
        target = jnp.where(live, rows, star_dev)
        positions = positions.at[:, target].set(new_pos, mode="drop")
        velocities = velocities.at[:, target].set(new_vel, mode="drop")
        accelerations = accelerations.at[:, target].set(own[:3], mode="drop")
        jerks = jerks.at[:, target].set(own[3:], mode="drop")
        last_time = last_time.at[target].set(now, mode="drop")
    return (positions, velocities, accelerations, jerks)


def solution(mesh):
    placed = (
        P(None, ("grp", "dev")),
        P(None, ("grp", "dev")),
        P(None, ("grp", "dev")),
        P(None, ("grp", "dev")),
        P(("grp", "dev")),
        P(),
        P(None, ("grp", "dev")),
    )
    return jax.shard_map(
        shards,
        mesh=mesh,
        in_specs=placed,
        out_specs=(
            P(None, ("grp", "dev")),
            P(None, ("grp", "dev")),
            P(None, ("grp", "dev")),
            P(None, ("grp", "dev")),
        ),
        check_vma=False,
    )
```

```python
import math

import jax
import jax.numpy as jnp
from jax import lax
from jax.experimental import pallas as pl
from jax.experimental.pallas import tpu as pltpu
from jax.sharding import PartitionSpec as P

tick_length = 1.0 / 128.0


LANES = 128
SUB = 8


def _pair_terms_kernel(n_ref, tgt_ref, src_ref, out_ref, *, soft_sq, mass, n_chunks):
    out_ref[...] = jnp.zeros(out_ref.shape, jnp.float32)

    def one_group(gi, carry):
        base = pl.multiple_of(gi * (2 * SUB), 2 * SUB)
        tile = tgt_ref[pl.ds(base, 2 * SUB), :]
        halves = []
        for h in range(2):
            part = tile[h * SUB:(h + 1) * SUB, :]
            halves.append([jnp.broadcast_to(part[:, k:k + 1], (SUB, LANES)) for k in range(6)])

        def chunk(c, accs):
            off = pl.multiple_of(c * LANES, LANES)
            s = [src_ref[k, :, pl.ds(off, LANES)] for k in range(6)]
            new = []
            for h in range(2):
                t = halves[h]
                a = accs[6 * h:6 * h + 6]
                dx = s[0] - t[0]
                dy = s[1] - t[1]
                dz = s[2] - t[2]
                ux = s[3] - t[3]
                uy = s[4] - t[4]
                uz = s[5] - t[5]
                r2 = dx * dx + dy * dy + dz * dz + soft_sq
                inv = lax.rsqrt(r2)
                inv2 = inv * inv
                w = inv * inv2
                al = 3.0 * (dx * ux + dy * uy + dz * uz) * inv2
                new += [
                    a[0] + w * dx,
                    a[1] + w * dy,
                    a[2] + w * dz,
                    a[3] + w * (ux - al * dx),
                    a[4] + w * (uy - al * dy),
                    a[5] + w * (uz - al * dz),
                ]
            return tuple(new)

        zero = jnp.zeros((SUB, LANES), jnp.float32)
        accs = lax.fori_loop(0, n_chunks, chunk, (zero,) * 12, unroll=2)
        for h in range(2):
            for k in range(6):
                total = jnp.sum(accs[6 * h + k], axis=1, keepdims=True) * mass
                out_ref[pl.ds(base + h * SUB, SUB), pl.ds(k, 1)] = total
        return carry

    lax.fori_loop(0, n_ref[0], one_group, 0)


def pair_terms(n_groups, tgt, src, mass, soft_sq, interpret=False):
    cap = tgt.shape[0]
    n_src = src.shape[1]
    src_b = jnp.broadcast_to(src[:, None, :], (6, SUB, n_src))
    kernel = lambda *refs: _pair_terms_kernel(*refs, soft_sq=soft_sq, mass=mass, n_chunks=n_src // LANES)
    return pl.pallas_call(
        kernel,
        out_shape=jax.ShapeDtypeStruct((cap, 8), jnp.float32),
        in_specs=[
            pl.BlockSpec(memory_space=pltpu.SMEM),
            pl.BlockSpec(memory_space=pltpu.VMEM),
            pl.BlockSpec(memory_space=pltpu.VMEM),
        ],
        out_specs=pl.BlockSpec(memory_space=pltpu.VMEM),
        interpret=interpret,
    )(jnp.reshape(n_groups, (1,)).astype(jnp.int32), tgt, src_b)


def pair_block(targets, src_pos, src_vel, mass, soft_sq):
    gap_x = src_pos[0][None, :] - targets[0][:, None]
    gap_y = src_pos[1][None, :] - targets[1][:, None]
    gap_z = src_pos[2][None, :] - targets[2][:, None]
    drift_x = src_vel[0][None, :] - targets[3][:, None]
    drift_y = src_vel[1][None, :] - targets[4][:, None]
    drift_z = src_vel[2][None, :] - targets[5][:, None]
    squared = gap_x * gap_x + gap_y * gap_y + gap_z * gap_z + soft_sq
    inverse = lax.rsqrt(squared)
    weight = mass * inverse * inverse * inverse
    along = 3.0 * (gap_x * drift_x + gap_y * drift_y + gap_z * drift_z) * inverse * inverse
    return jnp.stack(
        [
            jnp.sum(weight * gap_x, axis=1),
            jnp.sum(weight * gap_y, axis=1),
            jnp.sum(weight * gap_z, axis=1),
            jnp.sum(weight * (drift_x - along * gap_x), axis=1),
            jnp.sum(weight * (drift_y - along * gap_y), axis=1),
            jnp.sum(weight * (drift_z - along * gap_z), axis=1),
        ]
    )


def block_terms(packed, src_pos, src_vel, mass, soft_sq):
    width, total = packed.shape
    block = math.gcd(total, 2048)
    grouped = packed.reshape(width, total // block, block).transpose(1, 0, 2)
    result = lax.map(lambda targets: pair_block(targets, src_pos, src_vel, mass, soft_sq), grouped)
    return result.transpose(1, 0, 2).reshape(width, total)


def predict(positions, velocities, accelerations, jerks, elapsed):
    span = elapsed[None, :]
    pred_pos = (
        positions
        + span * velocities
        + 0.5 * span * span * accelerations
        + span * span * span / 6.0 * jerks
    )
    pred_vel = velocities + span * accelerations + 0.5 * span * span * jerks
    return (pred_pos, pred_vel)


def correct(old_pos, old_vel, old_acc, old_jerk, force, jerk_new, span):
    span = span[None, :]
    new_vel = old_vel + 0.5 * span * (old_acc + force) + span * span / 12.0 * (old_jerk - jerk_new)
    new_pos = old_pos + 0.5 * span * (old_vel + new_vel) + span * span / 12.0 * (old_acc - force)
    return (new_pos, new_vel)


def shards(positions, velocities, accelerations, jerks, levels, counts, active_rows):
    n_grp = lax.axis_size("grp")
    n_dev = lax.axis_size("dev")
    g_idx = lax.axis_index("grp")
    d_idx = lax.axis_index("dev")
    devices_all = n_grp * n_dev
    star_dev = positions.shape[1]
    slot_cap = active_rows.shape[1]
    stars_all = star_dev * devices_all
    mass = 1.0 / stars_all
    soft_sq = 0.0004 * (131072.0 / stars_all) ** (2.0 / 3.0)
    col_cap = n_grp * slot_cap
    last_time = -(jnp.left_shift(jnp.int32(1), levels) - 1).astype(jnp.float32) * tick_length
    for step in range(active_rows.shape[0]):
        now = (step + 1) * tick_length
        pred_pos, pred_vel = predict(positions, velocities, accelerations, jerks, now - last_time)
        rows = active_rows[step]
        targets = jnp.concatenate([pred_pos[:, rows], pred_vel[:, rows]], axis=0)
        col_counts = counts[step].reshape(n_grp, n_dev)[:, d_idx]
        inclusive = jnp.cumsum(col_counts).astype(jnp.int32)
        first = inclusive - col_counts
        col_live = inclusive[-1]
        place = jnp.arange(col_cap, dtype=jnp.int32)
        owner = jnp.sum((inclusive[None, :] <= place[:, None]).astype(jnp.int32), axis=1)
        owner = jnp.minimum(owner, n_grp - 1)
        slot = jnp.clip(owner * slot_cap + place - first[owner], 0, col_cap - 1)
        col_targets = lax.all_gather(targets, "grp", axis=1, tiled=True)
        padded = jnp.concatenate([col_targets, jnp.zeros((2, col_cap), jnp.float32)], axis=0)
        compact = padded.T[slot]
        src = lax.all_gather(jnp.concatenate([pred_pos, pred_vel], axis=0), "dev", axis=1, tiled=True)
        n_groups = (col_live + 2 * SUB - 1) // (2 * SUB)
        partial = pair_terms(n_groups, compact, src, mass, soft_sq)
        totals = lax.psum(partial[:, :6].T, "grp")
        totals = jnp.concatenate([totals, jnp.zeros((6, slot_cap), jnp.float32)], axis=1)
        own = lax.dynamic_slice_in_dim(totals, first[g_idx], slot_cap, 1)
        own_count = col_counts[g_idx]
        span = now - last_time[rows]
        new_pos, new_vel = correct(
            positions[:, rows],
            velocities[:, rows],
            accelerations[:, rows],
            jerks[:, rows],
            own[:3],
            own[3:],
            span,
        )
        live = jnp.arange(slot_cap, dtype=jnp.int32) < own_count
        target = jnp.where(live, rows, star_dev)
        positions = positions.at[:, target].set(new_pos, mode="drop")
        velocities = velocities.at[:, target].set(new_vel, mode="drop")
        accelerations = accelerations.at[:, target].set(own[:3], mode="drop")
        jerks = jerks.at[:, target].set(own[3:], mode="drop")
        last_time = last_time.at[target].set(now, mode="drop")
    return (positions, velocities, accelerations, jerks)


def solution(mesh):
    placed = (
        P(None, ("grp", "dev")),
        P(None, ("grp", "dev")),
        P(None, ("grp", "dev")),
        P(None, ("grp", "dev")),
        P(("grp", "dev")),
        P(),
        P(None, ("grp", "dev")),
    )
    return jax.shard_map(
        shards,
        mesh=mesh,
        in_specs=placed,
        out_specs=(
            P(None, ("grp", "dev")),
            P(None, ("grp", "dev")),
            P(None, ("grp", "dev")),
            P(None, ("grp", "dev")),
        ),
        check_vma=False,
    )
```

```python
import math

import jax
import jax.numpy as jnp
from jax import lax
from jax.experimental import pallas as pl
from jax.experimental.pallas import tpu as pltpu
from jax.sharding import PartitionSpec as P

tick_length = 1.0 / 128.0


LANES = 128
SUB = 8


def _pair_terms_kernel(cnt_ref, tgt_ref, src_ref, out_ref, *, soft_sq, mass, n_chunks, n_owner, slot_cap):
    out_ref[...] = jnp.zeros(out_ref.shape, jnp.float32)

    def one_group(base):
        tile = tgt_ref[pl.ds(base, 2 * SUB), :]
        halves = []
        for h in range(2):
            part = tile[h * SUB:(h + 1) * SUB, :]
            halves.append([jnp.broadcast_to(part[:, k:k + 1], (SUB, LANES)) for k in range(6)])

        def chunk(c, accs):
            off = pl.multiple_of(c * LANES, LANES)
            s = [src_ref[k, :, pl.ds(off, LANES)] for k in range(6)]
            new = []
            for h in range(2):
                t = halves[h]
                a = accs[6 * h:6 * h + 6]
                dx = s[0] - t[0]
                dy = s[1] - t[1]
                dz = s[2] - t[2]
                ux = s[3] - t[3]
                uy = s[4] - t[4]
                uz = s[5] - t[5]
                r2 = dx * dx + dy * dy + dz * dz + soft_sq
                inv = lax.rsqrt(r2)
                inv2 = inv * inv
                w = inv * inv2
                al = 3.0 * (dx * ux + dy * uy + dz * uz) * inv2
                new += [
                    a[0] + w * dx,
                    a[1] + w * dy,
                    a[2] + w * dz,
                    a[3] + w * (ux - al * dx),
                    a[4] + w * (uy - al * dy),
                    a[5] + w * (uz - al * dz),
                ]
            return tuple(new)

        zero = jnp.zeros((SUB, LANES), jnp.float32)
        accs = lax.fori_loop(0, n_chunks, chunk, (zero,) * 12, unroll=2)
        for h in range(2):
            for k in range(6):
                total = jnp.sum(accs[6 * h + k], axis=1, keepdims=True) * mass
                out_ref[pl.ds(base + h * SUB, SUB), pl.ds(k, 1)] = total

    def one_owner(o, carry):
        n_groups = (jnp.clip(cnt_ref[o], 0, slot_cap) + 2 * SUB - 1) // (2 * SUB)

        def body(gi, c):
            one_group(pl.multiple_of(o * slot_cap + gi * (2 * SUB), 2 * SUB))
            return c

        return lax.fori_loop(0, n_groups, body, carry)

    lax.fori_loop(0, n_owner, one_owner, 0)


def pair_terms(col_counts, tgt, src, mass, soft_sq, interpret=False):
    cap = tgt.shape[0]
    n_owner = col_counts.shape[0]
    n_src = src.shape[1]
    src_b = jnp.broadcast_to(src[:, None, :], (6, SUB, n_src))
    kernel = lambda *refs: _pair_terms_kernel(
        *refs, soft_sq=soft_sq, mass=mass, n_chunks=n_src // LANES, n_owner=n_owner, slot_cap=cap // n_owner
    )
    return pl.pallas_call(
        kernel,
        out_shape=jax.ShapeDtypeStruct((cap, 8), jnp.float32),
        in_specs=[
            pl.BlockSpec(memory_space=pltpu.SMEM),
            pl.BlockSpec(memory_space=pltpu.VMEM),
            pl.BlockSpec(memory_space=pltpu.VMEM),
        ],
        out_specs=pl.BlockSpec(memory_space=pltpu.VMEM),
        interpret=interpret,
    )(col_counts.astype(jnp.int32), tgt, src_b)


def pair_block(targets, src_pos, src_vel, mass, soft_sq):
    gap_x = src_pos[0][None, :] - targets[0][:, None]
    gap_y = src_pos[1][None, :] - targets[1][:, None]
    gap_z = src_pos[2][None, :] - targets[2][:, None]
    drift_x = src_vel[0][None, :] - targets[3][:, None]
    drift_y = src_vel[1][None, :] - targets[4][:, None]
    drift_z = src_vel[2][None, :] - targets[5][:, None]
    squared = gap_x * gap_x + gap_y * gap_y + gap_z * gap_z + soft_sq
    inverse = lax.rsqrt(squared)
    weight = mass * inverse * inverse * inverse
    along = 3.0 * (gap_x * drift_x + gap_y * drift_y + gap_z * drift_z) * inverse * inverse
    return jnp.stack(
        [
            jnp.sum(weight * gap_x, axis=1),
            jnp.sum(weight * gap_y, axis=1),
            jnp.sum(weight * gap_z, axis=1),
            jnp.sum(weight * (drift_x - along * gap_x), axis=1),
            jnp.sum(weight * (drift_y - along * gap_y), axis=1),
            jnp.sum(weight * (drift_z - along * gap_z), axis=1),
        ]
    )


def block_terms(packed, src_pos, src_vel, mass, soft_sq):
    width, total = packed.shape
    block = math.gcd(total, 2048)
    grouped = packed.reshape(width, total // block, block).transpose(1, 0, 2)
    result = lax.map(lambda targets: pair_block(targets, src_pos, src_vel, mass, soft_sq), grouped)
    return result.transpose(1, 0, 2).reshape(width, total)


def predict(positions, velocities, accelerations, jerks, elapsed):
    span = elapsed[None, :]
    pred_pos = (
        positions
        + span * velocities
        + 0.5 * span * span * accelerations
        + span * span * span / 6.0 * jerks
    )
    pred_vel = velocities + span * accelerations + 0.5 * span * span * jerks
    return (pred_pos, pred_vel)


def correct(old_pos, old_vel, old_acc, old_jerk, force, jerk_new, span):
    span = span[None, :]
    new_vel = old_vel + 0.5 * span * (old_acc + force) + span * span / 12.0 * (old_jerk - jerk_new)
    new_pos = old_pos + 0.5 * span * (old_vel + new_vel) + span * span / 12.0 * (old_acc - force)
    return (new_pos, new_vel)


def shards(positions, velocities, accelerations, jerks, levels, counts, active_rows):
    n_grp = lax.axis_size("grp")
    n_dev = lax.axis_size("dev")
    g_idx = lax.axis_index("grp")
    d_idx = lax.axis_index("dev")
    devices_all = n_grp * n_dev
    star_dev = positions.shape[1]
    slot_cap = active_rows.shape[1]
    stars_all = star_dev * devices_all
    mass = 1.0 / stars_all
    soft_sq = 0.0004 * (131072.0 / stars_all) ** (2.0 / 3.0)
    col_cap = n_grp * slot_cap
    last_time = -(jnp.left_shift(jnp.int32(1), levels) - 1).astype(jnp.float32) * tick_length
    for step in range(active_rows.shape[0]):
        now = (step + 1) * tick_length
        pred_pos, pred_vel = predict(positions, velocities, accelerations, jerks, now - last_time)
        rows = active_rows[step]
        targets = jnp.concatenate([pred_pos[:, rows], pred_vel[:, rows]], axis=0)
        col_counts = counts[step].reshape(n_grp, n_dev)[:, d_idx]
        col_targets = lax.all_gather(targets, "grp", axis=1, tiled=True)
        padded = jnp.concatenate([col_targets, jnp.zeros((2, col_cap), jnp.float32)], axis=0)
        src = lax.all_gather(jnp.concatenate([pred_pos, pred_vel], axis=0), "dev", axis=1, tiled=True)
        partial = pair_terms(col_counts, padded.T, src, mass, soft_sq)
        totals = lax.psum(partial[:, :6].T, "grp")
        own = lax.dynamic_slice_in_dim(totals, g_idx * slot_cap, slot_cap, 1)
        own_count = col_counts[g_idx]
        span = now - last_time[rows]
        new_pos, new_vel = correct(
            positions[:, rows],
            velocities[:, rows],
            accelerations[:, rows],
            jerks[:, rows],
            own[:3],
            own[3:],
            span,
        )
        live = jnp.arange(slot_cap, dtype=jnp.int32) < own_count
        target = jnp.where(live, rows, star_dev)
        positions = positions.at[:, target].set(new_pos, mode="drop")
        velocities = velocities.at[:, target].set(new_vel, mode="drop")
        accelerations = accelerations.at[:, target].set(own[:3], mode="drop")
        jerks = jerks.at[:, target].set(own[3:], mode="drop")
        last_time = last_time.at[target].set(now, mode="drop")
    return (positions, velocities, accelerations, jerks)


def solution(mesh):
    placed = (
        P(None, ("grp", "dev")),
        P(None, ("grp", "dev")),
        P(None, ("grp", "dev")),
        P(None, ("grp", "dev")),
        P(("grp", "dev")),
        P(),
        P(None, ("grp", "dev")),
    )
    return jax.shard_map(
        shards,
        mesh=mesh,
        in_specs=placed,
        out_specs=(
            P(None, ("grp", "dev")),
            P(None, ("grp", "dev")),
            P(None, ("grp", "dev")),
            P(None, ("grp", "dev")),
        ),
        check_vma=False,
    )
```

```python
import math

import jax
import jax.numpy as jnp
from jax import lax
from jax.experimental import pallas as pl
from jax.experimental.pallas import tpu as pltpu
from jax.sharding import PartitionSpec as P

tick_length = 1.0 / 128.0


LANES = 128
SUB = 8


def _pair_terms_kernel(cnt_ref, tgt_ref, src_ref, out_ref, *, soft_sq, mass, n_chunks, n_owner, slot_cap):
    out_ref[...] = jnp.zeros(out_ref.shape, jnp.float32)

    def one_group(base):
        tile = tgt_ref[pl.ds(base, 2 * SUB), :]
        halves = []
        for h in range(2):
            part = tile[h * SUB:(h + 1) * SUB, :]
            halves.append([jnp.broadcast_to(part[:, k:k + 1], (SUB, LANES)) for k in range(6)])

        def chunk(c, accs):
            off = pl.multiple_of(c * LANES, LANES)
            s = [src_ref[k, :, pl.ds(off, LANES)] for k in range(6)]
            new = []
            for h in range(2):
                t = halves[h]
                a = accs[6 * h:6 * h + 6]
                dx = s[0] - t[0]
                dy = s[1] - t[1]
                dz = s[2] - t[2]
                ux = s[3] - t[3]
                uy = s[4] - t[4]
                uz = s[5] - t[5]
                r2 = dx * dx + dy * dy + dz * dz + soft_sq
                inv = lax.rsqrt(r2)
                inv2 = inv * inv
                w = inv * inv2
                al = 3.0 * (dx * ux + dy * uy + dz * uz) * inv2
                new += [
                    a[0] + w * dx,
                    a[1] + w * dy,
                    a[2] + w * dz,
                    a[3] + w * (ux - al * dx),
                    a[4] + w * (uy - al * dy),
                    a[5] + w * (uz - al * dz),
                ]
            return tuple(new)

        zero = jnp.zeros((SUB, LANES), jnp.float32)
        accs = lax.fori_loop(0, n_chunks, chunk, (zero,) * 12, unroll=4)
        for h in range(2):
            for k in range(6):
                total = jnp.sum(accs[6 * h + k], axis=1, keepdims=True) * mass
                out_ref[pl.ds(base + h * SUB, SUB), pl.ds(k, 1)] = total

    def one_owner(o, carry):
        n_groups = (jnp.clip(cnt_ref[o], 0, slot_cap) + 2 * SUB - 1) // (2 * SUB)

        def body(gi, c):
            one_group(pl.multiple_of(o * slot_cap + gi * (2 * SUB), 2 * SUB))
            return c

        return lax.fori_loop(0, n_groups, body, carry)

    lax.fori_loop(0, n_owner, one_owner, 0)


def pair_terms(col_counts, tgt, src, mass, soft_sq, interpret=False):
    cap = tgt.shape[0]
    n_owner = col_counts.shape[0]
    n_src = src.shape[1]
    src_b = jnp.broadcast_to(src[:, None, :], (6, SUB, n_src))
    kernel = lambda *refs: _pair_terms_kernel(
        *refs, soft_sq=soft_sq, mass=mass, n_chunks=n_src // LANES, n_owner=n_owner, slot_cap=cap // n_owner
    )
    return pl.pallas_call(
        kernel,
        out_shape=jax.ShapeDtypeStruct((cap, 8), jnp.float32),
        in_specs=[
            pl.BlockSpec(memory_space=pltpu.SMEM),
            pl.BlockSpec(memory_space=pltpu.VMEM),
            pl.BlockSpec(memory_space=pltpu.VMEM),
        ],
        out_specs=pl.BlockSpec(memory_space=pltpu.VMEM),
        interpret=interpret,
    )(col_counts.astype(jnp.int32), tgt, src_b)


def pair_block(targets, src_pos, src_vel, mass, soft_sq):
    gap_x = src_pos[0][None, :] - targets[0][:, None]
    gap_y = src_pos[1][None, :] - targets[1][:, None]
    gap_z = src_pos[2][None, :] - targets[2][:, None]
    drift_x = src_vel[0][None, :] - targets[3][:, None]
    drift_y = src_vel[1][None, :] - targets[4][:, None]
    drift_z = src_vel[2][None, :] - targets[5][:, None]
    squared = gap_x * gap_x + gap_y * gap_y + gap_z * gap_z + soft_sq
    inverse = lax.rsqrt(squared)
    weight = mass * inverse * inverse * inverse
    along = 3.0 * (gap_x * drift_x + gap_y * drift_y + gap_z * drift_z) * inverse * inverse
    return jnp.stack(
        [
            jnp.sum(weight * gap_x, axis=1),
            jnp.sum(weight * gap_y, axis=1),
            jnp.sum(weight * gap_z, axis=1),
            jnp.sum(weight * (drift_x - along * gap_x), axis=1),
            jnp.sum(weight * (drift_y - along * gap_y), axis=1),
            jnp.sum(weight * (drift_z - along * gap_z), axis=1),
        ]
    )


def block_terms(packed, src_pos, src_vel, mass, soft_sq):
    width, total = packed.shape
    block = math.gcd(total, 2048)
    grouped = packed.reshape(width, total // block, block).transpose(1, 0, 2)
    result = lax.map(lambda targets: pair_block(targets, src_pos, src_vel, mass, soft_sq), grouped)
    return result.transpose(1, 0, 2).reshape(width, total)


def predict(positions, velocities, accelerations, jerks, elapsed):
    span = elapsed[None, :]
    pred_pos = (
        positions
        + span * velocities
        + 0.5 * span * span * accelerations
        + span * span * span / 6.0 * jerks
    )
    pred_vel = velocities + span * accelerations + 0.5 * span * span * jerks
    return (pred_pos, pred_vel)


def correct(old_pos, old_vel, old_acc, old_jerk, force, jerk_new, span):
    span = span[None, :]
    new_vel = old_vel + 0.5 * span * (old_acc + force) + span * span / 12.0 * (old_jerk - jerk_new)
    new_pos = old_pos + 0.5 * span * (old_vel + new_vel) + span * span / 12.0 * (old_acc - force)
    return (new_pos, new_vel)


def shards(positions, velocities, accelerations, jerks, levels, counts, active_rows):
    n_grp = lax.axis_size("grp")
    n_dev = lax.axis_size("dev")
    g_idx = lax.axis_index("grp")
    d_idx = lax.axis_index("dev")
    devices_all = n_grp * n_dev
    star_dev = positions.shape[1]
    slot_cap = active_rows.shape[1]
    stars_all = star_dev * devices_all
    mass = 1.0 / stars_all
    soft_sq = 0.0004 * (131072.0 / stars_all) ** (2.0 / 3.0)
    col_cap = n_grp * slot_cap
    last_time = -(jnp.left_shift(jnp.int32(1), levels) - 1).astype(jnp.float32) * tick_length
    for step in range(active_rows.shape[0]):
        now = (step + 1) * tick_length
        pred_pos, pred_vel = predict(positions, velocities, accelerations, jerks, now - last_time)
        rows = active_rows[step]
        targets = jnp.concatenate([pred_pos[:, rows], pred_vel[:, rows]], axis=0)
        col_counts = counts[step].reshape(n_grp, n_dev)[:, d_idx]
        col_targets = lax.all_gather(targets, "grp", axis=1, tiled=True)
        padded = jnp.concatenate([col_targets, jnp.zeros((2, col_cap), jnp.float32)], axis=0)
        src = lax.all_gather(jnp.concatenate([pred_pos, pred_vel], axis=0), "dev", axis=1, tiled=True)
        partial = pair_terms(col_counts, padded.T, src, mass, soft_sq)
        totals = lax.psum(partial[:, :6].T, "grp")
        own = lax.dynamic_slice_in_dim(totals, g_idx * slot_cap, slot_cap, 1)
        own_count = col_counts[g_idx]
        span = now - last_time[rows]
        new_pos, new_vel = correct(
            positions[:, rows],
            velocities[:, rows],
            accelerations[:, rows],
            jerks[:, rows],
            own[:3],
            own[3:],
            span,
        )
        live = jnp.arange(slot_cap, dtype=jnp.int32) < own_count
        target = jnp.where(live, rows, star_dev)
        positions = positions.at[:, target].set(new_pos, mode="drop")
        velocities = velocities.at[:, target].set(new_vel, mode="drop")
        accelerations = accelerations.at[:, target].set(own[:3], mode="drop")
        jerks = jerks.at[:, target].set(own[3:], mode="drop")
        last_time = last_time.at[target].set(now, mode="drop")
    return (positions, velocities, accelerations, jerks)


def solution(mesh):
    placed = (
        P(None, ("grp", "dev")),
        P(None, ("grp", "dev")),
        P(None, ("grp", "dev")),
        P(None, ("grp", "dev")),
        P(("grp", "dev")),
        P(),
        P(None, ("grp", "dev")),
    )
    return jax.shard_map(
        shards,
        mesh=mesh,
        in_specs=placed,
        out_specs=(
            P(None, ("grp", "dev")),
            P(None, ("grp", "dev")),
            P(None, ("grp", "dev")),
            P(None, ("grp", "dev")),
        ),
        check_vma=False,
    )
```

```python
import math

import jax
import jax.numpy as jnp
from jax import lax
from jax.experimental import pallas as pl
from jax.experimental.pallas import tpu as pltpu
from jax.sharding import PartitionSpec as P

tick_length = 1.0 / 128.0


LANES = 128
SUB = 8


def _pair_terms_kernel(cnt_ref, tgt_ref, src_ref, out_ref, *, soft_sq, mass, n_chunks, n_owner, slot_cap):
    out_ref[...] = jnp.zeros(out_ref.shape, jnp.float32)

    def one_group(base):
        tile = tgt_ref[pl.ds(base, 2 * SUB), :]
        halves = []
        for h in range(2):
            part = tile[h * SUB:(h + 1) * SUB, :]
            halves.append([jnp.broadcast_to(part[:, k:k + 1], (SUB, LANES)) for k in range(6)])

        def chunk(c, accs):
            off = pl.multiple_of(c * LANES, LANES)
            s = [src_ref[k, :, pl.ds(off, LANES)] for k in range(6)]
            new = []
            for h in range(2):
                t = halves[h]
                a = accs[6 * h:6 * h + 6]
                dx = s[0] - t[0]
                dy = s[1] - t[1]
                dz = s[2] - t[2]
                ux = s[3] - t[3]
                uy = s[4] - t[4]
                uz = s[5] - t[5]
                r2 = dx * dx + dy * dy + dz * dz + soft_sq
                inv = lax.rsqrt(r2)
                inv2 = inv * inv
                w = inv * inv2
                al = 3.0 * (dx * ux + dy * uy + dz * uz) * inv2
                new += [
                    a[0] + w * dx,
                    a[1] + w * dy,
                    a[2] + w * dz,
                    a[3] + w * (ux - al * dx),
                    a[4] + w * (uy - al * dy),
                    a[5] + w * (uz - al * dz),
                ]
            return tuple(new)

        zero = jnp.zeros((SUB, LANES), jnp.float32)
        accs = lax.fori_loop(0, n_chunks, chunk, (zero,) * 12, unroll=4)
        for h in range(2):
            for k in range(6):
                total = jnp.sum(accs[6 * h + k], axis=1, keepdims=True) * mass
                out_ref[pl.ds(base + h * SUB, SUB), pl.ds(k, 1)] = total

    def one_owner(o, carry):
        n_groups = (jnp.clip(cnt_ref[o], 0, slot_cap) + 2 * SUB - 1) // (2 * SUB)

        def body(gi, c):
            one_group(pl.multiple_of(o * slot_cap + gi * (2 * SUB), 2 * SUB))
            return c

        return lax.fori_loop(0, n_groups, body, carry)

    lax.fori_loop(0, n_owner, one_owner, 0)


def pair_terms(col_counts, tgt, src, mass, soft_sq, interpret=False):
    cap = tgt.shape[0]
    n_owner = col_counts.shape[0]
    n_src = src.shape[1]
    src_b = jnp.broadcast_to(src[:, None, :], (6, SUB, n_src))
    kernel = lambda *refs: _pair_terms_kernel(
        *refs, soft_sq=soft_sq, mass=mass, n_chunks=n_src // LANES, n_owner=n_owner, slot_cap=cap // n_owner
    )
    return pl.pallas_call(
        kernel,
        out_shape=jax.ShapeDtypeStruct((cap, 8), jnp.float32),
        in_specs=[
            pl.BlockSpec(memory_space=pltpu.SMEM),
            pl.BlockSpec(memory_space=pltpu.VMEM),
            pl.BlockSpec(memory_space=pltpu.VMEM),
        ],
        out_specs=pl.BlockSpec(memory_space=pltpu.VMEM),
        interpret=interpret,
    )(col_counts.astype(jnp.int32), tgt, src_b)


def pair_block(targets, src_pos, src_vel, mass, soft_sq):
    gap_x = src_pos[0][None, :] - targets[0][:, None]
    gap_y = src_pos[1][None, :] - targets[1][:, None]
    gap_z = src_pos[2][None, :] - targets[2][:, None]
    drift_x = src_vel[0][None, :] - targets[3][:, None]
    drift_y = src_vel[1][None, :] - targets[4][:, None]
    drift_z = src_vel[2][None, :] - targets[5][:, None]
    squared = gap_x * gap_x + gap_y * gap_y + gap_z * gap_z + soft_sq
    inverse = lax.rsqrt(squared)
    weight = mass * inverse * inverse * inverse
    along = 3.0 * (gap_x * drift_x + gap_y * drift_y + gap_z * drift_z) * inverse * inverse
    return jnp.stack(
        [
            jnp.sum(weight * gap_x, axis=1),
            jnp.sum(weight * gap_y, axis=1),
            jnp.sum(weight * gap_z, axis=1),
            jnp.sum(weight * (drift_x - along * gap_x), axis=1),
            jnp.sum(weight * (drift_y - along * gap_y), axis=1),
            jnp.sum(weight * (drift_z - along * gap_z), axis=1),
        ]
    )


def block_terms(packed, src_pos, src_vel, mass, soft_sq):
    width, total = packed.shape
    block = math.gcd(total, 2048)
    grouped = packed.reshape(width, total // block, block).transpose(1, 0, 2)
    result = lax.map(lambda targets: pair_block(targets, src_pos, src_vel, mass, soft_sq), grouped)
    return result.transpose(1, 0, 2).reshape(width, total)


def predict(positions, velocities, accelerations, jerks, elapsed):
    span = elapsed[None, :]
    pred_pos = (
        positions
        + span * velocities
        + 0.5 * span * span * accelerations
        + span * span * span / 6.0 * jerks
    )
    pred_vel = velocities + span * accelerations + 0.5 * span * span * jerks
    return (pred_pos, pred_vel)


def correct(old_pos, old_vel, old_acc, old_jerk, force, jerk_new, span):
    span = span[None, :]
    new_vel = old_vel + 0.5 * span * (old_acc + force) + span * span / 12.0 * (old_jerk - jerk_new)
    new_pos = old_pos + 0.5 * span * (old_vel + new_vel) + span * span / 12.0 * (old_acc - force)
    return (new_pos, new_vel)


def shards(positions, velocities, accelerations, jerks, levels, counts, active_rows):
    n_grp = lax.axis_size("grp")
    n_dev = lax.axis_size("dev")
    g_idx = lax.axis_index("grp")
    d_idx = lax.axis_index("dev")
    devices_all = n_grp * n_dev
    star_dev = positions.shape[1]
    slot_cap = active_rows.shape[1]
    stars_all = star_dev * devices_all
    mass = 1.0 / stars_all
    soft_sq = 0.0004 * (131072.0 / stars_all) ** (2.0 / 3.0)
    col_cap = n_grp * slot_cap
    last_time = -(jnp.left_shift(jnp.int32(1), levels) - 1).astype(jnp.float32) * tick_length
    for step in range(active_rows.shape[0]):
        now = (step + 1) * tick_length
        pred_pos, pred_vel = predict(positions, velocities, accelerations, jerks, now - last_time)
        rows = active_rows[step]
        targets = jnp.concatenate(
            [pred_pos[:, rows], pred_vel[:, rows], jnp.zeros((2, slot_cap), jnp.float32)], axis=0
        ).T
        col_counts = counts[step].reshape(n_grp, n_dev)[:, d_idx]
        packed = targets.reshape(slot_cap * 8 // LANES, LANES)
        col_targets = lax.all_gather(packed, "grp", axis=0, tiled=True).reshape(col_cap, 8)
        src = lax.all_gather(jnp.concatenate([pred_pos, pred_vel], axis=0), "dev", axis=1, tiled=True)
        partial = pair_terms(col_counts, col_targets, src, mass, soft_sq)
        dense = lax.optimization_barrier(partial.reshape(col_cap * 8 // LANES, LANES))
        totals = lax.optimization_barrier(lax.psum(dense, "grp")).reshape(col_cap, 8)
        own = lax.dynamic_slice_in_dim(totals, g_idx * slot_cap, slot_cap, 0)[:, :6].T
        own_count = col_counts[g_idx]
        span = now - last_time[rows]
        new_pos, new_vel = correct(
            positions[:, rows],
            velocities[:, rows],
            accelerations[:, rows],
            jerks[:, rows],
            own[:3],
            own[3:],
            span,
        )
        live = jnp.arange(slot_cap, dtype=jnp.int32) < own_count
        target = jnp.where(live, rows, star_dev)
        positions = positions.at[:, target].set(new_pos, mode="drop")
        velocities = velocities.at[:, target].set(new_vel, mode="drop")
        accelerations = accelerations.at[:, target].set(own[:3], mode="drop")
        jerks = jerks.at[:, target].set(own[3:], mode="drop")
        last_time = last_time.at[target].set(now, mode="drop")
    return (positions, velocities, accelerations, jerks)


def solution(mesh):
    placed = (
        P(None, ("grp", "dev")),
        P(None, ("grp", "dev")),
        P(None, ("grp", "dev")),
        P(None, ("grp", "dev")),
        P(("grp", "dev")),
        P(),
        P(None, ("grp", "dev")),
    )
    return jax.shard_map(
        shards,
        mesh=mesh,
        in_specs=placed,
        out_specs=(
            P(None, ("grp", "dev")),
            P(None, ("grp", "dev")),
            P(None, ("grp", "dev")),
            P(None, ("grp", "dev")),
        ),
        check_vma=False,
    )
```

```python
import math

import jax
import jax.numpy as jnp
from jax import lax
from jax.experimental import pallas as pl
from jax.experimental.pallas import tpu as pltpu
from jax.sharding import PartitionSpec as P

tick_length = 1.0 / 128.0


LANES = 128
SUB = 8


def _pair_terms_kernel(cnt_ref, tgt_ref, src_ref, out_ref, *, soft_sq, mass, n_chunks, n_owner, slot_cap):
    out_ref[...] = jnp.zeros(out_ref.shape, jnp.float32)

    def one_group(base):
        tile = tgt_ref[pl.ds(base, 2 * SUB), :]
        halves = []
        for h in range(2):
            part = tile[h * SUB:(h + 1) * SUB, :]
            halves.append([jnp.broadcast_to(part[:, k:k + 1], (SUB, LANES)) for k in range(6)])

        def chunk(c, accs):
            off = pl.multiple_of(c * LANES, LANES)
            s = [src_ref[k, :, pl.ds(off, LANES)] for k in range(6)]
            new = []
            for h in range(2):
                t = halves[h]
                a = accs[6 * h:6 * h + 6]
                dx = s[0] - t[0]
                dy = s[1] - t[1]
                dz = s[2] - t[2]
                ux = s[3] - t[3]
                uy = s[4] - t[4]
                uz = s[5] - t[5]
                r2 = dx * dx + dy * dy + dz * dz + soft_sq
                inv = lax.rsqrt(r2)
                inv2 = inv * inv
                w = inv * inv2
                al = 3.0 * (dx * ux + dy * uy + dz * uz) * inv2
                new += [
                    a[0] + w * dx,
                    a[1] + w * dy,
                    a[2] + w * dz,
                    a[3] + w * (ux - al * dx),
                    a[4] + w * (uy - al * dy),
                    a[5] + w * (uz - al * dz),
                ]
            return tuple(new)

        zero = jnp.zeros((SUB, LANES), jnp.float32)
        accs = lax.fori_loop(0, n_chunks, chunk, (zero,) * 12, unroll=4)
        for h in range(2):
            for k in range(6):
                total = jnp.sum(accs[6 * h + k], axis=1, keepdims=True) * mass
                out_ref[pl.ds(base + h * SUB, SUB), pl.ds(k, 1)] = total

    def one_owner(o, carry):
        n_groups = (jnp.clip(cnt_ref[o], 0, slot_cap) + 2 * SUB - 1) // (2 * SUB)

        def body(gi, c):
            one_group(pl.multiple_of(o * slot_cap + gi * (2 * SUB), 2 * SUB))
            return c

        return lax.fori_loop(0, n_groups, body, carry)

    lax.fori_loop(0, n_owner, one_owner, 0)


def pair_terms(col_counts, tgt, src, mass, soft_sq, interpret=False):
    cap = tgt.shape[0]
    n_owner = col_counts.shape[0]
    n_src = src.shape[1]
    src_b = jnp.broadcast_to(src[:, None, :], (6, SUB, n_src))
    kernel = lambda *refs: _pair_terms_kernel(
        *refs, soft_sq=soft_sq, mass=mass, n_chunks=n_src // LANES, n_owner=n_owner, slot_cap=cap // n_owner
    )
    return pl.pallas_call(
        kernel,
        out_shape=jax.ShapeDtypeStruct((cap, 8), jnp.float32),
        in_specs=[
            pl.BlockSpec(memory_space=pltpu.SMEM),
            pl.BlockSpec(memory_space=pltpu.VMEM),
            pl.BlockSpec(memory_space=pltpu.VMEM),
        ],
        out_specs=pl.BlockSpec(memory_space=pltpu.VMEM),
        interpret=interpret,
    )(col_counts.astype(jnp.int32), tgt, src_b)


def pair_block(targets, src_pos, src_vel, mass, soft_sq):
    gap_x = src_pos[0][None, :] - targets[0][:, None]
    gap_y = src_pos[1][None, :] - targets[1][:, None]
    gap_z = src_pos[2][None, :] - targets[2][:, None]
    drift_x = src_vel[0][None, :] - targets[3][:, None]
    drift_y = src_vel[1][None, :] - targets[4][:, None]
    drift_z = src_vel[2][None, :] - targets[5][:, None]
    squared = gap_x * gap_x + gap_y * gap_y + gap_z * gap_z + soft_sq
    inverse = lax.rsqrt(squared)
    weight = mass * inverse * inverse * inverse
    along = 3.0 * (gap_x * drift_x + gap_y * drift_y + gap_z * drift_z) * inverse * inverse
    return jnp.stack(
        [
            jnp.sum(weight * gap_x, axis=1),
            jnp.sum(weight * gap_y, axis=1),
            jnp.sum(weight * gap_z, axis=1),
            jnp.sum(weight * (drift_x - along * gap_x), axis=1),
            jnp.sum(weight * (drift_y - along * gap_y), axis=1),
            jnp.sum(weight * (drift_z - along * gap_z), axis=1),
        ]
    )


def block_terms(packed, src_pos, src_vel, mass, soft_sq):
    width, total = packed.shape
    block = math.gcd(total, 2048)
    grouped = packed.reshape(width, total // block, block).transpose(1, 0, 2)
    result = lax.map(lambda targets: pair_block(targets, src_pos, src_vel, mass, soft_sq), grouped)
    return result.transpose(1, 0, 2).reshape(width, total)


def predict(positions, velocities, accelerations, jerks, elapsed):
    span = elapsed[None, :]
    pred_pos = (
        positions
        + span * velocities
        + 0.5 * span * span * accelerations
        + span * span * span / 6.0 * jerks
    )
    pred_vel = velocities + span * accelerations + 0.5 * span * span * jerks
    return (pred_pos, pred_vel)


def correct(old_pos, old_vel, old_acc, old_jerk, force, jerk_new, span):
    span = span[None, :]
    new_vel = old_vel + 0.5 * span * (old_acc + force) + span * span / 12.0 * (old_jerk - jerk_new)
    new_pos = old_pos + 0.5 * span * (old_vel + new_vel) + span * span / 12.0 * (old_acc - force)
    return (new_pos, new_vel)


def shards(positions, velocities, accelerations, jerks, levels, counts, active_rows):
    n_grp = lax.axis_size("grp")
    n_dev = lax.axis_size("dev")
    g_idx = lax.axis_index("grp")
    d_idx = lax.axis_index("dev")
    devices_all = n_grp * n_dev
    star_dev = positions.shape[1]
    slot_cap = active_rows.shape[1]
    stars_all = star_dev * devices_all
    mass = 1.0 / stars_all
    soft_sq = 0.0004 * (131072.0 / stars_all) ** (2.0 / 3.0)
    col_cap = n_grp * slot_cap
    last_time = -(jnp.left_shift(jnp.int32(1), levels) - 1).astype(jnp.float32) * tick_length
    for step in range(active_rows.shape[0]):
        now = (step + 1) * tick_length
        pred_pos, pred_vel = predict(positions, velocities, accelerations, jerks, now - last_time)
        rows = active_rows[step]
        targets = jnp.concatenate(
            [pred_pos[:, rows], pred_vel[:, rows], jnp.zeros((2, slot_cap), jnp.float32)], axis=0
        ).T
        col_counts = counts[step].reshape(n_grp, n_dev)[:, d_idx]
        packed = targets.reshape(slot_cap * 8 // LANES, LANES)
        copies = lax.optimization_barrier(jnp.broadcast_to(packed[None], (n_grp,) + packed.shape))
        col_targets = lax.all_to_all(copies, "grp", 0, 0, tiled=True).reshape(col_cap, 8)
        src = lax.all_gather(jnp.concatenate([pred_pos, pred_vel], axis=0), "dev", axis=1, tiled=True)
        partial = pair_terms(col_counts, col_targets, src, mass, soft_sq)
        chunks = lax.optimization_barrier(partial.reshape(n_grp, slot_cap * 8 // LANES, LANES))
        received = lax.all_to_all(chunks, "grp", 0, 0, tiled=True)
        own = jnp.sum(received, axis=0).reshape(slot_cap, 8)[:, :6].T
        own_count = col_counts[g_idx]
        span = now - last_time[rows]
        new_pos, new_vel = correct(
            positions[:, rows],
            velocities[:, rows],
            accelerations[:, rows],
            jerks[:, rows],
            own[:3],
            own[3:],
            span,
        )
        live = jnp.arange(slot_cap, dtype=jnp.int32) < own_count
        target = jnp.where(live, rows, star_dev)
        positions = positions.at[:, target].set(new_pos, mode="drop")
        velocities = velocities.at[:, target].set(new_vel, mode="drop")
        accelerations = accelerations.at[:, target].set(own[:3], mode="drop")
        jerks = jerks.at[:, target].set(own[3:], mode="drop")
        last_time = last_time.at[target].set(now, mode="drop")
    return (positions, velocities, accelerations, jerks)


def solution(mesh):
    placed = (
        P(None, ("grp", "dev")),
        P(None, ("grp", "dev")),
        P(None, ("grp", "dev")),
        P(None, ("grp", "dev")),
        P(("grp", "dev")),
        P(),
        P(None, ("grp", "dev")),
    )
    return jax.shard_map(
        shards,
        mesh=mesh,
        in_specs=placed,
        out_specs=(
            P(None, ("grp", "dev")),
            P(None, ("grp", "dev")),
            P(None, ("grp", "dev")),
            P(None, ("grp", "dev")),
        ),
        check_vma=False,
    )
```

```python
import math

import jax
import jax.numpy as jnp
from jax import lax
from jax.experimental import pallas as pl
from jax.experimental.pallas import tpu as pltpu
from jax.sharding import PartitionSpec as P

tick_length = 1.0 / 128.0


LANES = 128
SUB = 8


def _pair_terms_kernel(cnt_ref, tgt_ref, src_ref, out_ref, *, soft_sq, mass, n_chunks, n_owner, slot_cap):
    out_ref[...] = jnp.zeros(out_ref.shape, jnp.float32)

    def one_group(base):
        tile = tgt_ref[pl.ds(base, 2 * SUB), :]
        halves = []
        for h in range(2):
            part = tile[h * SUB:(h + 1) * SUB, :]
            halves.append([jnp.broadcast_to(part[:, k:k + 1], (SUB, LANES)) for k in range(6)])

        def chunk(c, accs):
            off = pl.multiple_of(c * LANES, LANES)
            s = [src_ref[k, :, pl.ds(off, LANES)] for k in range(6)]
            new = []
            for h in range(2):
                t = halves[h]
                a = accs[6 * h:6 * h + 6]
                dx = s[0] - t[0]
                dy = s[1] - t[1]
                dz = s[2] - t[2]
                ux = s[3] - t[3]
                uy = s[4] - t[4]
                uz = s[5] - t[5]
                r2 = dx * dx + dy * dy + dz * dz + soft_sq
                inv = lax.rsqrt(r2)
                inv2 = inv * inv
                w = inv * inv2
                al = 3.0 * (dx * ux + dy * uy + dz * uz) * inv2
                new += [
                    a[0] + w * dx,
                    a[1] + w * dy,
                    a[2] + w * dz,
                    a[3] + w * (ux - al * dx),
                    a[4] + w * (uy - al * dy),
                    a[5] + w * (uz - al * dz),
                ]
            return tuple(new)

        zero = jnp.zeros((SUB, LANES), jnp.float32)
        accs = lax.fori_loop(0, n_chunks, chunk, (zero,) * 12, unroll=4)
        for h in range(2):
            for k in range(6):
                total = jnp.sum(accs[6 * h + k], axis=1, keepdims=True) * mass
                out_ref[pl.ds(base + h * SUB, SUB), pl.ds(k, 1)] = total

    def one_owner(o, carry):
        n_groups = (jnp.clip(cnt_ref[o], 0, slot_cap) + 2 * SUB - 1) // (2 * SUB)

        def body(gi, c):
            one_group(pl.multiple_of(o * slot_cap + gi * (2 * SUB), 2 * SUB))
            return c

        return lax.fori_loop(0, n_groups, body, carry)

    lax.fori_loop(0, n_owner, one_owner, 0)


def pair_terms(col_counts, tgt, src, mass, soft_sq, interpret=False):
    cap = tgt.shape[0]
    n_owner = col_counts.shape[0]
    n_src = src.shape[1]
    src_b = jnp.broadcast_to(src[:, None, :], (6, SUB, n_src))
    kernel = lambda *refs: _pair_terms_kernel(
        *refs, soft_sq=soft_sq, mass=mass, n_chunks=n_src // LANES, n_owner=n_owner, slot_cap=cap // n_owner
    )
    return pl.pallas_call(
        kernel,
        out_shape=jax.ShapeDtypeStruct((cap, 8), jnp.float32),
        in_specs=[
            pl.BlockSpec(memory_space=pltpu.SMEM),
            pl.BlockSpec(memory_space=pltpu.VMEM),
            pl.BlockSpec(memory_space=pltpu.VMEM),
        ],
        out_specs=pl.BlockSpec(memory_space=pltpu.VMEM),
        interpret=interpret,
    )(col_counts.astype(jnp.int32), tgt, src_b)


def pair_block(targets, src_pos, src_vel, mass, soft_sq):
    gap_x = src_pos[0][None, :] - targets[0][:, None]
    gap_y = src_pos[1][None, :] - targets[1][:, None]
    gap_z = src_pos[2][None, :] - targets[2][:, None]
    drift_x = src_vel[0][None, :] - targets[3][:, None]
    drift_y = src_vel[1][None, :] - targets[4][:, None]
    drift_z = src_vel[2][None, :] - targets[5][:, None]
    squared = gap_x * gap_x + gap_y * gap_y + gap_z * gap_z + soft_sq
    inverse = lax.rsqrt(squared)
    weight = mass * inverse * inverse * inverse
    along = 3.0 * (gap_x * drift_x + gap_y * drift_y + gap_z * drift_z) * inverse * inverse
    return jnp.stack(
        [
            jnp.sum(weight * gap_x, axis=1),
            jnp.sum(weight * gap_y, axis=1),
            jnp.sum(weight * gap_z, axis=1),
            jnp.sum(weight * (drift_x - along * gap_x), axis=1),
            jnp.sum(weight * (drift_y - along * gap_y), axis=1),
            jnp.sum(weight * (drift_z - along * gap_z), axis=1),
        ]
    )


def block_terms(packed, src_pos, src_vel, mass, soft_sq):
    width, total = packed.shape
    block = math.gcd(total, 2048)
    grouped = packed.reshape(width, total // block, block).transpose(1, 0, 2)
    result = lax.map(lambda targets: pair_block(targets, src_pos, src_vel, mass, soft_sq), grouped)
    return result.transpose(1, 0, 2).reshape(width, total)


def predict(positions, velocities, accelerations, jerks, elapsed):
    span = elapsed[None, :]
    pred_pos = (
        positions
        + span * velocities
        + 0.5 * span * span * accelerations
        + span * span * span / 6.0 * jerks
    )
    pred_vel = velocities + span * accelerations + 0.5 * span * span * jerks
    return (pred_pos, pred_vel)


def correct(old_pos, old_vel, old_acc, old_jerk, force, jerk_new, span):
    span = span[None, :]
    new_vel = old_vel + 0.5 * span * (old_acc + force) + span * span / 12.0 * (old_jerk - jerk_new)
    new_pos = old_pos + 0.5 * span * (old_vel + new_vel) + span * span / 12.0 * (old_acc - force)
    return (new_pos, new_vel)


def shards(positions, velocities, accelerations, jerks, levels, counts, active_rows):
    n_grp = lax.axis_size("grp")
    n_dev = lax.axis_size("dev")
    g_idx = lax.axis_index("grp")
    d_idx = lax.axis_index("dev")
    devices_all = n_grp * n_dev
    star_dev = positions.shape[1]
    slot_cap = active_rows.shape[1]
    stars_all = star_dev * devices_all
    mass = 1.0 / stars_all
    soft_sq = 0.0004 * (131072.0 / stars_all) ** (2.0 / 3.0)
    col_cap = n_grp * slot_cap
    last_time = -(jnp.left_shift(jnp.int32(1), levels) - 1).astype(jnp.float32) * tick_length
    for step in range(active_rows.shape[0]):
        now = (step + 1) * tick_length
        pred_pos, pred_vel = predict(positions, velocities, accelerations, jerks, now - last_time)
        rows = active_rows[step]
        targets = jnp.concatenate(
            [pred_pos[:, rows], pred_vel[:, rows], jnp.zeros((2, slot_cap), jnp.float32)], axis=0
        ).T
        col_counts = counts[step].reshape(n_grp, n_dev)[:, d_idx]
        packed = targets.reshape(slot_cap * 8 // LANES, LANES)
        copies = lax.optimization_barrier(jnp.broadcast_to(packed[None], (n_grp,) + packed.shape))
        col_targets = lax.all_to_all(copies, "grp", 0, 0, tiled=True).reshape(col_cap, 8)
        mine = jnp.concatenate([pred_pos, pred_vel], axis=0)
        spread = lax.optimization_barrier(jnp.broadcast_to(mine[None], (n_dev,) + mine.shape))
        src = lax.all_to_all(spread, "dev", 0, 0, tiled=True)
        src = src.transpose(1, 0, 2).reshape(6, n_dev * star_dev)
        partial = pair_terms(col_counts, col_targets, src, mass, soft_sq)
        chunks = lax.optimization_barrier(partial.reshape(n_grp, slot_cap * 8 // LANES, LANES))
        received = lax.all_to_all(chunks, "grp", 0, 0, tiled=True)
        own = jnp.sum(received, axis=0).reshape(slot_cap, 8)[:, :6].T
        own_count = col_counts[g_idx]
        span = now - last_time[rows]
        new_pos, new_vel = correct(
            positions[:, rows],
            velocities[:, rows],
            accelerations[:, rows],
            jerks[:, rows],
            own[:3],
            own[3:],
            span,
        )
        live = jnp.arange(slot_cap, dtype=jnp.int32) < own_count
        target = jnp.where(live, rows, star_dev)
        positions = positions.at[:, target].set(new_pos, mode="drop")
        velocities = velocities.at[:, target].set(new_vel, mode="drop")
        accelerations = accelerations.at[:, target].set(own[:3], mode="drop")
        jerks = jerks.at[:, target].set(own[3:], mode="drop")
        last_time = last_time.at[target].set(now, mode="drop")
    return (positions, velocities, accelerations, jerks)


def solution(mesh):
    placed = (
        P(None, ("grp", "dev")),
        P(None, ("grp", "dev")),
        P(None, ("grp", "dev")),
        P(None, ("grp", "dev")),
        P(("grp", "dev")),
        P(),
        P(None, ("grp", "dev")),
    )
    return jax.shard_map(
        shards,
        mesh=mesh,
        in_specs=placed,
        out_specs=(
            P(None, ("grp", "dev")),
            P(None, ("grp", "dev")),
            P(None, ("grp", "dev")),
            P(None, ("grp", "dev")),
        ),
        check_vma=False,
    )
```

```python
import math

import jax
import jax.numpy as jnp
from jax import lax
from jax.experimental import pallas as pl
from jax.experimental.pallas import tpu as pltpu
from jax.sharding import PartitionSpec as P

tick_length = 1.0 / 128.0


LANES = 128
SUB = 8


def _pair_terms_kernel(cnt_ref, tgt_ref, src_ref, out_ref, *, soft_sq, mass, n_chunks, n_owner, slot_cap):
    out_ref[...] = jnp.zeros(out_ref.shape, jnp.float32)

    def one_group(base):
        tile = tgt_ref[pl.ds(base, 2 * SUB), :]
        halves = []
        for h in range(2):
            part = tile[h * SUB:(h + 1) * SUB, :]
            halves.append([jnp.broadcast_to(part[:, k:k + 1], (SUB, LANES)) for k in range(6)])

        def chunk(c, accs):
            off = pl.multiple_of(c * LANES, LANES)
            s = [src_ref[k, :, pl.ds(off, LANES)] for k in range(6)]
            new = []
            for h in range(2):
                t = halves[h]
                a = accs[6 * h:6 * h + 6]
                dx = s[0] - t[0]
                dy = s[1] - t[1]
                dz = s[2] - t[2]
                ux = s[3] - t[3]
                uy = s[4] - t[4]
                uz = s[5] - t[5]
                r2 = dx * dx + dy * dy + dz * dz + soft_sq
                inv = lax.rsqrt(r2)
                inv2 = inv * inv
                w = inv * inv2
                al = 3.0 * (dx * ux + dy * uy + dz * uz) * inv2
                new += [
                    a[0] + w * dx,
                    a[1] + w * dy,
                    a[2] + w * dz,
                    a[3] + w * (ux - al * dx),
                    a[4] + w * (uy - al * dy),
                    a[5] + w * (uz - al * dz),
                ]
            return tuple(new)

        zero = jnp.zeros((SUB, LANES), jnp.float32)
        accs = lax.fori_loop(0, n_chunks, chunk, (zero,) * 12, unroll=4)
        for h in range(2):
            for k in range(6):
                total = jnp.sum(accs[6 * h + k], axis=1, keepdims=True) * mass
                out_ref[pl.ds(base + h * SUB, SUB), pl.ds(k, 1)] = total

    def one_owner(o, carry):
        n_groups = (jnp.clip(cnt_ref[o], 0, slot_cap) + 2 * SUB - 1) // (2 * SUB)

        def body(gi, c):
            one_group(pl.multiple_of(o * slot_cap + gi * (2 * SUB), 2 * SUB))
            return c

        return lax.fori_loop(0, n_groups, body, carry)

    lax.fori_loop(0, n_owner, one_owner, 0)


def pair_terms(col_counts, tgt, src, mass, soft_sq, interpret=False):
    cap = tgt.shape[0]
    n_owner = col_counts.shape[0]
    n_src = src.shape[1]
    src_b = jnp.broadcast_to(src[:, None, :], (6, SUB, n_src))
    kernel = lambda *refs: _pair_terms_kernel(
        *refs, soft_sq=soft_sq, mass=mass, n_chunks=n_src // LANES, n_owner=n_owner, slot_cap=cap // n_owner
    )
    return pl.pallas_call(
        kernel,
        out_shape=jax.ShapeDtypeStruct((cap, 8), jnp.float32),
        in_specs=[
            pl.BlockSpec(memory_space=pltpu.SMEM),
            pl.BlockSpec(memory_space=pltpu.VMEM),
            pl.BlockSpec(memory_space=pltpu.VMEM),
        ],
        out_specs=pl.BlockSpec(memory_space=pltpu.VMEM),
        interpret=interpret,
    )(col_counts.astype(jnp.int32), tgt, src_b)


def pair_block(targets, src_pos, src_vel, mass, soft_sq):
    gap_x = src_pos[0][None, :] - targets[0][:, None]
    gap_y = src_pos[1][None, :] - targets[1][:, None]
    gap_z = src_pos[2][None, :] - targets[2][:, None]
    drift_x = src_vel[0][None, :] - targets[3][:, None]
    drift_y = src_vel[1][None, :] - targets[4][:, None]
    drift_z = src_vel[2][None, :] - targets[5][:, None]
    squared = gap_x * gap_x + gap_y * gap_y + gap_z * gap_z + soft_sq
    inverse = lax.rsqrt(squared)
    weight = mass * inverse * inverse * inverse
    along = 3.0 * (gap_x * drift_x + gap_y * drift_y + gap_z * drift_z) * inverse * inverse
    return jnp.stack(
        [
            jnp.sum(weight * gap_x, axis=1),
            jnp.sum(weight * gap_y, axis=1),
            jnp.sum(weight * gap_z, axis=1),
            jnp.sum(weight * (drift_x - along * gap_x), axis=1),
            jnp.sum(weight * (drift_y - along * gap_y), axis=1),
            jnp.sum(weight * (drift_z - along * gap_z), axis=1),
        ]
    )


def block_terms(packed, src_pos, src_vel, mass, soft_sq):
    width, total = packed.shape
    block = math.gcd(total, 2048)
    grouped = packed.reshape(width, total // block, block).transpose(1, 0, 2)
    result = lax.map(lambda targets: pair_block(targets, src_pos, src_vel, mass, soft_sq), grouped)
    return result.transpose(1, 0, 2).reshape(width, total)


def predict(positions, velocities, accelerations, jerks, elapsed):
    span = elapsed[None, :]
    pred_pos = (
        positions
        + span * velocities
        + 0.5 * span * span * accelerations
        + span * span * span / 6.0 * jerks
    )
    pred_vel = velocities + span * accelerations + 0.5 * span * span * jerks
    return (pred_pos, pred_vel)


def correct(old_pos, old_vel, old_acc, old_jerk, force, jerk_new, span):
    span = span[None, :]
    new_vel = old_vel + 0.5 * span * (old_acc + force) + span * span / 12.0 * (old_jerk - jerk_new)
    new_pos = old_pos + 0.5 * span * (old_vel + new_vel) + span * span / 12.0 * (old_acc - force)
    return (new_pos, new_vel)


def shards(positions, velocities, accelerations, jerks, levels, counts, active_rows):
    n_grp = lax.axis_size("grp")
    n_dev = lax.axis_size("dev")
    g_idx = lax.axis_index("grp")
    d_idx = lax.axis_index("dev")
    devices_all = n_grp * n_dev
    star_dev = positions.shape[1]
    slot_cap = active_rows.shape[1]
    stars_all = star_dev * devices_all
    mass = 1.0 / stars_all
    soft_sq = 0.0004 * (131072.0 / stars_all) ** (2.0 / 3.0)
    row_cap = n_dev * slot_cap
    last_time = -(jnp.left_shift(jnp.int32(1), levels) - 1).astype(jnp.float32) * tick_length
    for step in range(active_rows.shape[0]):
        now = (step + 1) * tick_length
        pred_pos, pred_vel = predict(positions, velocities, accelerations, jerks, now - last_time)
        rows = active_rows[step]
        targets = jnp.concatenate(
            [pred_pos[:, rows], pred_vel[:, rows], jnp.zeros((2, slot_cap), jnp.float32)], axis=0
        ).T
        row_counts = counts[step].reshape(n_grp, n_dev)[g_idx, :]
        packed = targets.reshape(slot_cap * 8 // LANES, LANES)
        copies = lax.optimization_barrier(jnp.broadcast_to(packed[None], (n_dev,) + packed.shape))
        row_targets = lax.all_to_all(copies, "dev", 0, 0, tiled=True).reshape(row_cap, 8)
        mine = jnp.concatenate([pred_pos, pred_vel], axis=0)
        spread = lax.optimization_barrier(jnp.broadcast_to(mine[None], (n_grp,) + mine.shape))
        src = lax.all_to_all(spread, "grp", 0, 0, tiled=True)
        src = src.transpose(1, 0, 2).reshape(6, n_grp * star_dev)
        partial = pair_terms(row_counts, row_targets, src, mass, soft_sq)
        chunks = lax.optimization_barrier(partial.reshape(n_dev, slot_cap * 8 // LANES, LANES))
        received = lax.all_to_all(chunks, "dev", 0, 0, tiled=True)
        own = jnp.sum(received, axis=0).reshape(slot_cap, 8)[:, :6].T
        own_count = row_counts[d_idx]
        span = now - last_time[rows]
        new_pos, new_vel = correct(
            positions[:, rows],
            velocities[:, rows],
            accelerations[:, rows],
            jerks[:, rows],
            own[:3],
            own[3:],
            span,
        )
        live = jnp.arange(slot_cap, dtype=jnp.int32) < own_count
        target = jnp.where(live, rows, star_dev)
        positions = positions.at[:, target].set(new_pos, mode="drop")
        velocities = velocities.at[:, target].set(new_vel, mode="drop")
        accelerations = accelerations.at[:, target].set(own[:3], mode="drop")
        jerks = jerks.at[:, target].set(own[3:], mode="drop")
        last_time = last_time.at[target].set(now, mode="drop")
    return (positions, velocities, accelerations, jerks)


def solution(mesh):
    placed = (
        P(None, ("grp", "dev")),
        P(None, ("grp", "dev")),
        P(None, ("grp", "dev")),
        P(None, ("grp", "dev")),
        P(("grp", "dev")),
        P(),
        P(None, ("grp", "dev")),
    )
    return jax.shard_map(
        shards,
        mesh=mesh,
        in_specs=placed,
        out_specs=(
            P(None, ("grp", "dev")),
            P(None, ("grp", "dev")),
            P(None, ("grp", "dev")),
            P(None, ("grp", "dev")),
        ),
        check_vma=False,
    )
```

```python
import math

import jax
import jax.numpy as jnp
from jax import lax
from jax.experimental import pallas as pl
from jax.experimental.pallas import tpu as pltpu
from jax.sharding import PartitionSpec as P

tick_length = 1.0 / 128.0


LANES = 128
SUB = 8


def _pair_terms_kernel(cnt_ref, tgt_ref, src_ref, out_ref, *, soft_sq, mass, n_chunks, n_owner, slot_cap):
    out_ref[...] = jnp.zeros(out_ref.shape, jnp.float32)

    def one_group(base):
        tile = tgt_ref[pl.ds(base, 2 * SUB), :]
        halves = []
        for h in range(2):
            part = tile[h * SUB:(h + 1) * SUB, :]
            halves.append([jnp.broadcast_to(part[:, k:k + 1], (SUB, LANES)) for k in range(6)])

        def chunk(c, accs):
            off = pl.multiple_of(c * LANES, LANES)
            s = [src_ref[k, :, pl.ds(off, LANES)] for k in range(6)]
            new = []
            for h in range(2):
                t = halves[h]
                a = accs[6 * h:6 * h + 6]
                dx = s[0] - t[0]
                dy = s[1] - t[1]
                dz = s[2] - t[2]
                ux = s[3] - t[3]
                uy = s[4] - t[4]
                uz = s[5] - t[5]
                r2 = dx * dx + dy * dy + dz * dz + soft_sq
                inv = lax.rsqrt(r2)
                inv2 = inv * inv
                w = inv * inv2
                al = 3.0 * (dx * ux + dy * uy + dz * uz) * inv2
                new += [
                    a[0] + w * dx,
                    a[1] + w * dy,
                    a[2] + w * dz,
                    a[3] + w * (ux - al * dx),
                    a[4] + w * (uy - al * dy),
                    a[5] + w * (uz - al * dz),
                ]
            return tuple(new)

        zero = jnp.zeros((SUB, LANES), jnp.float32)
        accs = lax.fori_loop(0, n_chunks, chunk, (zero,) * 12, unroll=16)
        for h in range(2):
            for k in range(6):
                total = jnp.sum(accs[6 * h + k], axis=1, keepdims=True) * mass
                out_ref[pl.ds(base + h * SUB, SUB), pl.ds(k, 1)] = total

    def one_owner(o, carry):
        n_groups = (jnp.clip(cnt_ref[o], 0, slot_cap) + 2 * SUB - 1) // (2 * SUB)

        def body(gi, c):
            one_group(pl.multiple_of(o * slot_cap + gi * (2 * SUB), 2 * SUB))
            return c

        return lax.fori_loop(0, n_groups, body, carry)

    lax.fori_loop(0, n_owner, one_owner, 0)


def pair_terms(col_counts, tgt, src, mass, soft_sq, interpret=False):
    cap = tgt.shape[0]
    n_owner = col_counts.shape[0]
    n_src = src.shape[1]
    src_b = jnp.broadcast_to(src[:, None, :], (6, SUB, n_src))
    kernel = lambda *refs: _pair_terms_kernel(
        *refs, soft_sq=soft_sq, mass=mass, n_chunks=n_src // LANES, n_owner=n_owner, slot_cap=cap // n_owner
    )
    return pl.pallas_call(
        kernel,
        out_shape=jax.ShapeDtypeStruct((cap, 8), jnp.float32),
        in_specs=[
            pl.BlockSpec(memory_space=pltpu.SMEM),
            pl.BlockSpec(memory_space=pltpu.VMEM),
            pl.BlockSpec(memory_space=pltpu.VMEM),
        ],
        out_specs=pl.BlockSpec(memory_space=pltpu.VMEM),
        interpret=interpret,
    )(col_counts.astype(jnp.int32), tgt, src_b)


def pair_block(targets, src_pos, src_vel, mass, soft_sq):
    gap_x = src_pos[0][None, :] - targets[0][:, None]
    gap_y = src_pos[1][None, :] - targets[1][:, None]
    gap_z = src_pos[2][None, :] - targets[2][:, None]
    drift_x = src_vel[0][None, :] - targets[3][:, None]
    drift_y = src_vel[1][None, :] - targets[4][:, None]
    drift_z = src_vel[2][None, :] - targets[5][:, None]
    squared = gap_x * gap_x + gap_y * gap_y + gap_z * gap_z + soft_sq
    inverse = lax.rsqrt(squared)
    weight = mass * inverse * inverse * inverse
    along = 3.0 * (gap_x * drift_x + gap_y * drift_y + gap_z * drift_z) * inverse * inverse
    return jnp.stack(
        [
            jnp.sum(weight * gap_x, axis=1),
            jnp.sum(weight * gap_y, axis=1),
            jnp.sum(weight * gap_z, axis=1),
            jnp.sum(weight * (drift_x - along * gap_x), axis=1),
            jnp.sum(weight * (drift_y - along * gap_y), axis=1),
            jnp.sum(weight * (drift_z - along * gap_z), axis=1),
        ]
    )


def block_terms(packed, src_pos, src_vel, mass, soft_sq):
    width, total = packed.shape
    block = math.gcd(total, 2048)
    grouped = packed.reshape(width, total // block, block).transpose(1, 0, 2)
    result = lax.map(lambda targets: pair_block(targets, src_pos, src_vel, mass, soft_sq), grouped)
    return result.transpose(1, 0, 2).reshape(width, total)


def predict(positions, velocities, accelerations, jerks, elapsed):
    span = elapsed[None, :]
    pred_pos = (
        positions
        + span * velocities
        + 0.5 * span * span * accelerations
        + span * span * span / 6.0 * jerks
    )
    pred_vel = velocities + span * accelerations + 0.5 * span * span * jerks
    return (pred_pos, pred_vel)


def correct(old_pos, old_vel, old_acc, old_jerk, force, jerk_new, span):
    span = span[None, :]
    new_vel = old_vel + 0.5 * span * (old_acc + force) + span * span / 12.0 * (old_jerk - jerk_new)
    new_pos = old_pos + 0.5 * span * (old_vel + new_vel) + span * span / 12.0 * (old_acc - force)
    return (new_pos, new_vel)


def shards(positions, velocities, accelerations, jerks, levels, counts, active_rows):
    n_grp = lax.axis_size("grp")
    n_dev = lax.axis_size("dev")
    g_idx = lax.axis_index("grp")
    d_idx = lax.axis_index("dev")
    devices_all = n_grp * n_dev
    star_dev = positions.shape[1]
    slot_cap = active_rows.shape[1]
    stars_all = star_dev * devices_all
    mass = 1.0 / stars_all
    soft_sq = 0.0004 * (131072.0 / stars_all) ** (2.0 / 3.0)
    row_cap = n_dev * slot_cap
    last_time = -(jnp.left_shift(jnp.int32(1), levels) - 1).astype(jnp.float32) * tick_length
    for step in range(active_rows.shape[0]):
        now = (step + 1) * tick_length
        pred_pos, pred_vel = predict(positions, velocities, accelerations, jerks, now - last_time)
        rows = active_rows[step]
        targets = jnp.concatenate(
            [pred_pos[:, rows], pred_vel[:, rows], jnp.zeros((2, slot_cap), jnp.float32)], axis=0
        ).T
        row_counts = counts[step].reshape(n_grp, n_dev)[g_idx, :]
        packed = targets.reshape(slot_cap * 8 // LANES, LANES)
        copies = lax.optimization_barrier(jnp.broadcast_to(packed[None], (n_dev,) + packed.shape))
        row_targets = lax.all_to_all(copies, "dev", 0, 0, tiled=True).reshape(row_cap, 8)
        mine = jnp.concatenate([pred_pos, pred_vel], axis=0)
        spread = lax.optimization_barrier(jnp.broadcast_to(mine[None], (n_grp,) + mine.shape))
        src = lax.all_to_all(spread, "grp", 0, 0, tiled=True)
        src = src.transpose(1, 0, 2).reshape(6, n_grp * star_dev)
        partial = pair_terms(row_counts, row_targets, src, mass, soft_sq)
        chunks = lax.optimization_barrier(partial.reshape(n_dev, slot_cap * 8 // LANES, LANES))
        received = lax.all_to_all(chunks, "dev", 0, 0, tiled=True)
        own = jnp.sum(received, axis=0).reshape(slot_cap, 8)[:, :6].T
        own_count = row_counts[d_idx]
        span = now - last_time[rows]
        new_pos, new_vel = correct(
            positions[:, rows],
            velocities[:, rows],
            accelerations[:, rows],
            jerks[:, rows],
            own[:3],
            own[3:],
            span,
        )
        live = jnp.arange(slot_cap, dtype=jnp.int32) < own_count
        target = jnp.where(live, rows, star_dev)
        positions = positions.at[:, target].set(new_pos, mode="drop")
        velocities = velocities.at[:, target].set(new_vel, mode="drop")
        accelerations = accelerations.at[:, target].set(own[:3], mode="drop")
        jerks = jerks.at[:, target].set(own[3:], mode="drop")
        last_time = last_time.at[target].set(now, mode="drop")
    return (positions, velocities, accelerations, jerks)


def solution(mesh):
    placed = (
        P(None, ("grp", "dev")),
        P(None, ("grp", "dev")),
        P(None, ("grp", "dev")),
        P(None, ("grp", "dev")),
        P(("grp", "dev")),
        P(),
        P(None, ("grp", "dev")),
    )
    return jax.shard_map(
        shards,
        mesh=mesh,
        in_specs=placed,
        out_specs=(
            P(None, ("grp", "dev")),
            P(None, ("grp", "dev")),
            P(None, ("grp", "dev")),
            P(None, ("grp", "dev")),
        ),
        check_vma=False,
    )
```

```python
import math

import jax
import jax.numpy as jnp
from jax import lax
from jax.experimental import pallas as pl
from jax.experimental.pallas import tpu as pltpu
from jax.sharding import PartitionSpec as P

tick_length = 1.0 / 128.0


LANES = 128
SUB = 8


def _pair_terms_kernel(cnt_ref, tgt_ref, src_ref, out_ref, *, soft_sq, mass, n_chunks, n_owner, slot_cap):
    out_ref[...] = jnp.zeros(out_ref.shape, jnp.float32)

    def one_group(base):
        tile = tgt_ref[pl.ds(base, 2 * SUB), :]
        halves = []
        for h in range(2):
            part = tile[h * SUB:(h + 1) * SUB, :]
            halves.append([jnp.broadcast_to(part[:, k:k + 1], (SUB, LANES)) for k in range(6)])

        def chunk(c, accs):
            off = pl.multiple_of(c * LANES, LANES)
            s = [src_ref[k, :, pl.ds(off, LANES)] for k in range(6)]
            new = []
            for h in range(2):
                t = halves[h]
                a = accs[6 * h:6 * h + 6]
                dx = s[0] - t[0]
                dy = s[1] - t[1]
                dz = s[2] - t[2]
                ux = s[3] - t[3]
                uy = s[4] - t[4]
                uz = s[5] - t[5]
                r2 = dx * dx + dy * dy + dz * dz + soft_sq
                inv = lax.rsqrt(r2)
                inv2 = inv * inv
                w = inv * inv2
                al = 3.0 * (dx * ux + dy * uy + dz * uz) * inv2
                new += [
                    a[0] + w * dx,
                    a[1] + w * dy,
                    a[2] + w * dz,
                    a[3] + w * (ux - al * dx),
                    a[4] + w * (uy - al * dy),
                    a[5] + w * (uz - al * dz),
                ]
            return tuple(new)

        zero = jnp.zeros((SUB, LANES), jnp.float32)
        accs = lax.fori_loop(0, n_chunks, chunk, (zero,) * 12, unroll=16)
        for h in range(2):
            for k in range(6):
                total = jnp.sum(accs[6 * h + k], axis=1, keepdims=True) * mass
                out_ref[pl.ds(base + h * SUB, SUB), pl.ds(k, 1)] = total

    def one_owner(o, carry):
        n_groups = (jnp.clip(cnt_ref[o], 0, slot_cap) + 2 * SUB - 1) // (2 * SUB)

        def body(gi, c):
            one_group(pl.multiple_of(o * slot_cap + gi * (2 * SUB), 2 * SUB))
            return c

        return lax.fori_loop(0, n_groups, body, carry)

    lax.fori_loop(0, n_owner, one_owner, 0)


def pair_terms(col_counts, tgt, src, mass, soft_sq, interpret=False):
    cap = tgt.shape[0]
    n_owner = col_counts.shape[0]
    n_src = src.shape[1]
    src_b = jnp.broadcast_to(src[:, None, :], (6, SUB, n_src))
    kernel = lambda *refs: _pair_terms_kernel(
        *refs, soft_sq=soft_sq, mass=mass, n_chunks=n_src // LANES, n_owner=n_owner, slot_cap=cap // n_owner
    )
    return pl.pallas_call(
        kernel,
        out_shape=jax.ShapeDtypeStruct((cap, 8), jnp.float32),
        in_specs=[
            pl.BlockSpec(memory_space=pltpu.SMEM),
            pl.BlockSpec(memory_space=pltpu.VMEM),
            pl.BlockSpec(memory_space=pltpu.VMEM),
        ],
        out_specs=pl.BlockSpec(memory_space=pltpu.VMEM),
        interpret=interpret,
    )(col_counts.astype(jnp.int32), tgt, src_b)


def pair_block(targets, src_pos, src_vel, mass, soft_sq):
    gap_x = src_pos[0][None, :] - targets[0][:, None]
    gap_y = src_pos[1][None, :] - targets[1][:, None]
    gap_z = src_pos[2][None, :] - targets[2][:, None]
    drift_x = src_vel[0][None, :] - targets[3][:, None]
    drift_y = src_vel[1][None, :] - targets[4][:, None]
    drift_z = src_vel[2][None, :] - targets[5][:, None]
    squared = gap_x * gap_x + gap_y * gap_y + gap_z * gap_z + soft_sq
    inverse = lax.rsqrt(squared)
    weight = mass * inverse * inverse * inverse
    along = 3.0 * (gap_x * drift_x + gap_y * drift_y + gap_z * drift_z) * inverse * inverse
    return jnp.stack(
        [
            jnp.sum(weight * gap_x, axis=1),
            jnp.sum(weight * gap_y, axis=1),
            jnp.sum(weight * gap_z, axis=1),
            jnp.sum(weight * (drift_x - along * gap_x), axis=1),
            jnp.sum(weight * (drift_y - along * gap_y), axis=1),
            jnp.sum(weight * (drift_z - along * gap_z), axis=1),
        ]
    )


def block_terms(packed, src_pos, src_vel, mass, soft_sq):
    width, total = packed.shape
    block = math.gcd(total, 2048)
    grouped = packed.reshape(width, total // block, block).transpose(1, 0, 2)
    result = lax.map(lambda targets: pair_block(targets, src_pos, src_vel, mass, soft_sq), grouped)
    return result.transpose(1, 0, 2).reshape(width, total)


def predict(positions, velocities, accelerations, jerks, elapsed):
    span = elapsed[None, :]
    pred_pos = (
        positions
        + span * velocities
        + 0.5 * span * span * accelerations
        + span * span * span / 6.0 * jerks
    )
    pred_vel = velocities + span * accelerations + 0.5 * span * span * jerks
    return (pred_pos, pred_vel)


def correct(old_pos, old_vel, old_acc, old_jerk, force, jerk_new, span):
    span = span[None, :]
    new_vel = old_vel + 0.5 * span * (old_acc + force) + span * span / 12.0 * (old_jerk - jerk_new)
    new_pos = old_pos + 0.5 * span * (old_vel + new_vel) + span * span / 12.0 * (old_acc - force)
    return (new_pos, new_vel)


def shards(positions, velocities, accelerations, jerks, levels, counts, active_rows):
    n_grp = lax.axis_size("grp")
    n_dev = lax.axis_size("dev")
    g_idx = lax.axis_index("grp")
    d_idx = lax.axis_index("dev")
    devices_all = n_grp * n_dev
    star_dev = positions.shape[1]
    slot_cap = active_rows.shape[1]
    stars_all = star_dev * devices_all
    mass = 1.0 / stars_all
    soft_sq = 0.0004 * (131072.0 / stars_all) ** (2.0 / 3.0)
    row_cap = n_dev * slot_cap
    last_time = -(jnp.left_shift(jnp.int32(1), levels) - 1).astype(jnp.float32) * tick_length
    state = jnp.concatenate([positions, velocities, accelerations, jerks], axis=0)
    for step in range(active_rows.shape[0]):
        now = (step + 1) * tick_length
        pred_pos, pred_vel = predict(state[0:3], state[3:6], state[6:9], state[9:12], now - last_time)
        rows = active_rows[step]
        targets = jnp.concatenate(
            [pred_pos[:, rows], pred_vel[:, rows], jnp.zeros((2, slot_cap), jnp.float32)], axis=0
        ).T
        row_counts = counts[step].reshape(n_grp, n_dev)[g_idx, :]
        packed = targets.reshape(slot_cap * 8 // LANES, LANES)
        copies = lax.optimization_barrier(jnp.broadcast_to(packed[None], (n_dev,) + packed.shape))
        row_targets = lax.all_to_all(copies, "dev", 0, 0, tiled=True).reshape(row_cap, 8)
        mine = jnp.concatenate([pred_pos, pred_vel], axis=0)
        spread = lax.optimization_barrier(jnp.broadcast_to(mine[None], (n_grp,) + mine.shape))
        src = lax.all_to_all(spread, "grp", 0, 0, tiled=True)
        src = src.transpose(1, 0, 2).reshape(6, n_grp * star_dev)
        partial = pair_terms(row_counts, row_targets, src, mass, soft_sq)
        chunks = lax.optimization_barrier(partial.reshape(n_dev, slot_cap * 8 // LANES, LANES))
        received = lax.all_to_all(chunks, "dev", 0, 0, tiled=True)
        own = jnp.sum(received, axis=0).reshape(slot_cap, 8)[:, :6].T
        own_count = row_counts[d_idx]
        span = now - last_time[rows]
        old = state[:, rows]
        new_pos, new_vel = correct(old[0:3], old[3:6], old[6:9], old[9:12], own[:3], own[3:], span)
        live = jnp.arange(slot_cap, dtype=jnp.int32) < own_count
        target = jnp.where(live, rows, star_dev)
        state = state.at[:, target].set(jnp.concatenate([new_pos, new_vel, own], axis=0), mode="drop")
        last_time = last_time.at[target].set(now, mode="drop")
    return (state[0:3], state[3:6], state[6:9], state[9:12])


def solution(mesh):
    placed = (
        P(None, ("grp", "dev")),
        P(None, ("grp", "dev")),
        P(None, ("grp", "dev")),
        P(None, ("grp", "dev")),
        P(("grp", "dev")),
        P(),
        P(None, ("grp", "dev")),
    )
    return jax.shard_map(
        shards,
        mesh=mesh,
        in_specs=placed,
        out_specs=(
            P(None, ("grp", "dev")),
            P(None, ("grp", "dev")),
            P(None, ("grp", "dev")),
            P(None, ("grp", "dev")),
        ),
        check_vma=False,
    )
```

```python
import math

import jax
import jax.numpy as jnp
from jax import lax
from jax.experimental import pallas as pl
from jax.experimental.pallas import tpu as pltpu
from jax.sharding import PartitionSpec as P

tick_length = 1.0 / 128.0


LANES = 128
SUB = 8


def _pair_terms_kernel(cnt_ref, tgt_ref, src_ref, out_ref, *, soft_sq, mass, n_chunks, n_owner, slot_cap):
    out_ref[...] = jnp.zeros(out_ref.shape, jnp.float32)

    def one_group(base, n_half):
        tile = tgt_ref[pl.ds(base, n_half * SUB), :]
        halves = []
        for h in range(n_half):
            part = tile[h * SUB:(h + 1) * SUB, :]
            halves.append([jnp.broadcast_to(part[:, k:k + 1], (SUB, LANES)) for k in range(6)])

        def chunk(c, accs):
            off = pl.multiple_of(c * LANES, LANES)
            s = [src_ref[k, :, pl.ds(off, LANES)] for k in range(6)]
            new = []
            for h in range(n_half):
                t = halves[h]
                a = accs[6 * h:6 * h + 6]
                dx = s[0] - t[0]
                dy = s[1] - t[1]
                dz = s[2] - t[2]
                ux = s[3] - t[3]
                uy = s[4] - t[4]
                uz = s[5] - t[5]
                r2 = dx * dx + dy * dy + dz * dz + soft_sq
                inv = lax.rsqrt(r2)
                inv2 = inv * inv
                w = inv * inv2
                al = 3.0 * (dx * ux + dy * uy + dz * uz) * inv2
                new += [
                    a[0] + w * dx,
                    a[1] + w * dy,
                    a[2] + w * dz,
                    a[3] + w * (ux - al * dx),
                    a[4] + w * (uy - al * dy),
                    a[5] + w * (uz - al * dz),
                ]
            return tuple(new)

        zero = jnp.zeros((SUB, LANES), jnp.float32)
        accs = lax.fori_loop(0, n_chunks, chunk, (zero,) * (6 * n_half), unroll=16)
        for h in range(n_half):
            for k in range(6):
                total = jnp.sum(accs[6 * h + k], axis=1, keepdims=True) * mass
                out_ref[pl.ds(base + h * SUB, SUB), pl.ds(k, 1)] = total

    def one_owner(o, carry):
        count = jnp.clip(cnt_ref[o], 0, slot_cap)
        n_full = count // (2 * SUB)
        rest = count - n_full * (2 * SUB)
        tail = pl.multiple_of(o * slot_cap + n_full * (2 * SUB), SUB)

        def body(gi, c):
            one_group(pl.multiple_of(o * slot_cap + gi * (2 * SUB), 2 * SUB), 2)
            return c

        lax.fori_loop(0, n_full, body, 0)

        @pl.when(rest > SUB)
        def _():
            one_group(tail, 2)

        @pl.when((rest > 0) & (rest <= SUB))
        def _():
            one_group(tail, 1)

        return carry

    lax.fori_loop(0, n_owner, one_owner, 0)


def pair_terms(col_counts, tgt, src, mass, soft_sq, interpret=False):
    cap = tgt.shape[0]
    n_owner = col_counts.shape[0]
    n_src = src.shape[1]
    src_b = jnp.broadcast_to(src[:, None, :], (6, SUB, n_src))
    kernel = lambda *refs: _pair_terms_kernel(
        *refs, soft_sq=soft_sq, mass=mass, n_chunks=n_src // LANES, n_owner=n_owner, slot_cap=cap // n_owner
    )
    return pl.pallas_call(
        kernel,
        out_shape=jax.ShapeDtypeStruct((cap, 8), jnp.float32),
        in_specs=[
            pl.BlockSpec(memory_space=pltpu.SMEM),
            pl.BlockSpec(memory_space=pltpu.VMEM),
            pl.BlockSpec(memory_space=pltpu.VMEM),
        ],
        out_specs=pl.BlockSpec(memory_space=pltpu.VMEM),
        interpret=interpret,
    )(col_counts.astype(jnp.int32), tgt, src_b)


def pair_block(targets, src_pos, src_vel, mass, soft_sq):
    gap_x = src_pos[0][None, :] - targets[0][:, None]
    gap_y = src_pos[1][None, :] - targets[1][:, None]
    gap_z = src_pos[2][None, :] - targets[2][:, None]
    drift_x = src_vel[0][None, :] - targets[3][:, None]
    drift_y = src_vel[1][None, :] - targets[4][:, None]
    drift_z = src_vel[2][None, :] - targets[5][:, None]
    squared = gap_x * gap_x + gap_y * gap_y + gap_z * gap_z + soft_sq
    inverse = lax.rsqrt(squared)
    weight = mass * inverse * inverse * inverse
    along = 3.0 * (gap_x * drift_x + gap_y * drift_y + gap_z * drift_z) * inverse * inverse
    return jnp.stack(
        [
            jnp.sum(weight * gap_x, axis=1),
            jnp.sum(weight * gap_y, axis=1),
            jnp.sum(weight * gap_z, axis=1),
            jnp.sum(weight * (drift_x - along * gap_x), axis=1),
            jnp.sum(weight * (drift_y - along * gap_y), axis=1),
            jnp.sum(weight * (drift_z - along * gap_z), axis=1),
        ]
    )


def block_terms(packed, src_pos, src_vel, mass, soft_sq):
    width, total = packed.shape
    block = math.gcd(total, 2048)
    grouped = packed.reshape(width, total // block, block).transpose(1, 0, 2)
    result = lax.map(lambda targets: pair_block(targets, src_pos, src_vel, mass, soft_sq), grouped)
    return result.transpose(1, 0, 2).reshape(width, total)


def predict(positions, velocities, accelerations, jerks, elapsed):
    span = elapsed[None, :]
    pred_pos = (
        positions
        + span * velocities
        + 0.5 * span * span * accelerations
        + span * span * span / 6.0 * jerks
    )
    pred_vel = velocities + span * accelerations + 0.5 * span * span * jerks
    return (pred_pos, pred_vel)


def correct(old_pos, old_vel, old_acc, old_jerk, force, jerk_new, span):
    span = span[None, :]
    new_vel = old_vel + 0.5 * span * (old_acc + force) + span * span / 12.0 * (old_jerk - jerk_new)
    new_pos = old_pos + 0.5 * span * (old_vel + new_vel) + span * span / 12.0 * (old_acc - force)
    return (new_pos, new_vel)


def shards(positions, velocities, accelerations, jerks, levels, counts, active_rows):
    n_grp = lax.axis_size("grp")
    n_dev = lax.axis_size("dev")
    g_idx = lax.axis_index("grp")
    d_idx = lax.axis_index("dev")
    devices_all = n_grp * n_dev
    star_dev = positions.shape[1]
    slot_cap = active_rows.shape[1]
    stars_all = star_dev * devices_all
    mass = 1.0 / stars_all
    soft_sq = 0.0004 * (131072.0 / stars_all) ** (2.0 / 3.0)
    row_cap = n_dev * slot_cap
    last_time = -(jnp.left_shift(jnp.int32(1), levels) - 1).astype(jnp.float32) * tick_length
    state = jnp.concatenate([positions, velocities, accelerations, jerks], axis=0)
    for step in range(active_rows.shape[0]):
        now = (step + 1) * tick_length
        pred_pos, pred_vel = predict(state[0:3], state[3:6], state[6:9], state[9:12], now - last_time)
        rows = active_rows[step]
        targets = jnp.concatenate(
            [pred_pos[:, rows], pred_vel[:, rows], jnp.zeros((2, slot_cap), jnp.float32)], axis=0
        ).T
        row_counts = counts[step].reshape(n_grp, n_dev)[g_idx, :]
        packed = targets.reshape(slot_cap * 8 // LANES, LANES)
        copies = lax.optimization_barrier(jnp.broadcast_to(packed[None], (n_dev,) + packed.shape))
        row_targets = lax.all_to_all(copies, "dev", 0, 0, tiled=True).reshape(row_cap, 8)
        mine = jnp.concatenate([pred_pos, pred_vel], axis=0)
        spread = lax.optimization_barrier(jnp.broadcast_to(mine[None], (n_grp,) + mine.shape))
        src = lax.all_to_all(spread, "grp", 0, 0, tiled=True)
        src = src.transpose(1, 0, 2).reshape(6, n_grp * star_dev)
        partial = pair_terms(row_counts, row_targets, src, mass, soft_sq)
        chunks = lax.optimization_barrier(partial.reshape(n_dev, slot_cap * 8 // LANES, LANES))
        received = lax.all_to_all(chunks, "dev", 0, 0, tiled=True)
        own = jnp.sum(received, axis=0).reshape(slot_cap, 8)[:, :6].T
        own_count = row_counts[d_idx]
        span = now - last_time[rows]
        old = state[:, rows]
        new_pos, new_vel = correct(old[0:3], old[3:6], old[6:9], old[9:12], own[:3], own[3:], span)
        live = jnp.arange(slot_cap, dtype=jnp.int32) < own_count
        target = jnp.where(live, rows, star_dev)
        state = state.at[:, target].set(jnp.concatenate([new_pos, new_vel, own], axis=0), mode="drop")
        last_time = last_time.at[target].set(now, mode="drop")
    return (state[0:3], state[3:6], state[6:9], state[9:12])


def solution(mesh):
    placed = (
        P(None, ("grp", "dev")),
        P(None, ("grp", "dev")),
        P(None, ("grp", "dev")),
        P(None, ("grp", "dev")),
        P(("grp", "dev")),
        P(),
        P(None, ("grp", "dev")),
    )
    return jax.shard_map(
        shards,
        mesh=mesh,
        in_specs=placed,
        out_specs=(
            P(None, ("grp", "dev")),
            P(None, ("grp", "dev")),
            P(None, ("grp", "dev")),
            P(None, ("grp", "dev")),
        ),
        check_vma=False,
    )
```

```python
import math

import jax
import jax.numpy as jnp
from jax import lax
from jax.experimental import pallas as pl
from jax.experimental.pallas import tpu as pltpu
from jax.sharding import PartitionSpec as P

tick_length = 1.0 / 128.0


LANES = 128
SUB = 8


def _pair_terms_kernel(cnt_ref, tgt_ref, src_ref, out_ref, acc_ref, *, soft_sq, mass, n_chunks, n_owner, slot_cap):
    acc_ref[...] = jnp.zeros(acc_ref.shape, jnp.float32)

    def one_group(base, n_half):
        tile = tgt_ref[pl.ds(base, n_half * SUB), :]
        halves = []
        for h in range(n_half):
            part = tile[h * SUB:(h + 1) * SUB, :]
            halves.append([jnp.broadcast_to(part[:, k:k + 1], (SUB, LANES)) for k in range(6)])

        def chunk(c, accs):
            off = pl.multiple_of(c * LANES, LANES)
            s = [src_ref[k, :, pl.ds(off, LANES)] for k in range(6)]
            new = []
            for h in range(n_half):
                t = halves[h]
                a = accs[6 * h:6 * h + 6]
                dx = s[0] - t[0]
                dy = s[1] - t[1]
                dz = s[2] - t[2]
                ux = s[3] - t[3]
                uy = s[4] - t[4]
                uz = s[5] - t[5]
                r2 = dx * dx + dy * dy + dz * dz + soft_sq
                inv = lax.rsqrt(r2)
                inv2 = inv * inv
                w = inv * inv2
                al = 3.0 * (dx * ux + dy * uy + dz * uz) * inv2
                new += [
                    a[0] + w * dx,
                    a[1] + w * dy,
                    a[2] + w * dz,
                    a[3] + w * (ux - al * dx),
                    a[4] + w * (uy - al * dy),
                    a[5] + w * (uz - al * dz),
                ]
            return tuple(new)

        zero = jnp.zeros((SUB, LANES), jnp.float32)
        accs = lax.fori_loop(0, n_chunks, chunk, (zero,) * (6 * n_half), unroll=16)
        for h in range(n_half):
            for k in range(6):
                total = jnp.sum(accs[6 * h + k], axis=1, keepdims=True) * mass
                acc_ref[pl.ds(base + h * SUB, SUB), pl.ds(k, 1)] = total

    def one_owner(o, carry):
        count = jnp.clip(cnt_ref[o], 0, slot_cap)
        n_full = count // (2 * SUB)
        rest = count - n_full * (2 * SUB)
        tail = pl.multiple_of(o * slot_cap + n_full * (2 * SUB), SUB)

        def body(gi, c):
            one_group(pl.multiple_of(o * slot_cap + gi * (2 * SUB), 2 * SUB), 2)
            return c

        lax.fori_loop(0, n_full, body, 0)

        @pl.when(rest > SUB)
        def _():
            one_group(tail, 2)

        @pl.when((rest > 0) & (rest <= SUB))
        def _():
            one_group(tail, 1)

        return carry

    lax.fori_loop(0, n_owner, one_owner, 0)

    def flip(o, carry):
        block = acc_ref[pl.ds(pl.multiple_of(o * slot_cap, slot_cap), slot_cap), :]
        out_ref[o] = block.T[:8, :]
        return carry

    lax.fori_loop(0, n_owner, flip, 0)


def pair_terms(col_counts, tgt, src, mass, soft_sq, interpret=False):
    cap = tgt.shape[0]
    n_owner = col_counts.shape[0]
    n_src = src.shape[1]
    src_b = jnp.broadcast_to(src[:, None, :], (6, SUB, n_src))
    kernel = lambda *refs: _pair_terms_kernel(
        *refs, soft_sq=soft_sq, mass=mass, n_chunks=n_src // LANES, n_owner=n_owner, slot_cap=cap // n_owner
    )
    return pl.pallas_call(
        kernel,
        out_shape=jax.ShapeDtypeStruct((n_owner, 8, cap // n_owner), jnp.float32),
        in_specs=[
            pl.BlockSpec(memory_space=pltpu.SMEM),
            pl.BlockSpec(memory_space=pltpu.VMEM),
            pl.BlockSpec(memory_space=pltpu.VMEM),
        ],
        out_specs=pl.BlockSpec(memory_space=pltpu.VMEM),
        scratch_shapes=[pltpu.VMEM((cap, LANES), jnp.float32)],
        interpret=interpret,
    )(col_counts.astype(jnp.int32), tgt, src_b)


def pair_block(targets, src_pos, src_vel, mass, soft_sq):
    gap_x = src_pos[0][None, :] - targets[0][:, None]
    gap_y = src_pos[1][None, :] - targets[1][:, None]
    gap_z = src_pos[2][None, :] - targets[2][:, None]
    drift_x = src_vel[0][None, :] - targets[3][:, None]
    drift_y = src_vel[1][None, :] - targets[4][:, None]
    drift_z = src_vel[2][None, :] - targets[5][:, None]
    squared = gap_x * gap_x + gap_y * gap_y + gap_z * gap_z + soft_sq
    inverse = lax.rsqrt(squared)
    weight = mass * inverse * inverse * inverse
    along = 3.0 * (gap_x * drift_x + gap_y * drift_y + gap_z * drift_z) * inverse * inverse
    return jnp.stack(
        [
            jnp.sum(weight * gap_x, axis=1),
            jnp.sum(weight * gap_y, axis=1),
            jnp.sum(weight * gap_z, axis=1),
            jnp.sum(weight * (drift_x - along * gap_x), axis=1),
            jnp.sum(weight * (drift_y - along * gap_y), axis=1),
            jnp.sum(weight * (drift_z - along * gap_z), axis=1),
        ]
    )


def block_terms(packed, src_pos, src_vel, mass, soft_sq):
    width, total = packed.shape
    block = math.gcd(total, 2048)
    grouped = packed.reshape(width, total // block, block).transpose(1, 0, 2)
    result = lax.map(lambda targets: pair_block(targets, src_pos, src_vel, mass, soft_sq), grouped)
    return result.transpose(1, 0, 2).reshape(width, total)


def predict(positions, velocities, accelerations, jerks, elapsed):
    span = elapsed[None, :]
    pred_pos = (
        positions
        + span * velocities
        + 0.5 * span * span * accelerations
        + span * span * span / 6.0 * jerks
    )
    pred_vel = velocities + span * accelerations + 0.5 * span * span * jerks
    return (pred_pos, pred_vel)


def correct(old_pos, old_vel, old_acc, old_jerk, force, jerk_new, span):
    span = span[None, :]
    new_vel = old_vel + 0.5 * span * (old_acc + force) + span * span / 12.0 * (old_jerk - jerk_new)
    new_pos = old_pos + 0.5 * span * (old_vel + new_vel) + span * span / 12.0 * (old_acc - force)
    return (new_pos, new_vel)


def shards(positions, velocities, accelerations, jerks, levels, counts, active_rows):
    n_grp = lax.axis_size("grp")
    n_dev = lax.axis_size("dev")
    g_idx = lax.axis_index("grp")
    d_idx = lax.axis_index("dev")
    devices_all = n_grp * n_dev
    star_dev = positions.shape[1]
    slot_cap = active_rows.shape[1]
    stars_all = star_dev * devices_all
    mass = 1.0 / stars_all
    soft_sq = 0.0004 * (131072.0 / stars_all) ** (2.0 / 3.0)
    row_cap = n_dev * slot_cap
    last_time = -(jnp.left_shift(jnp.int32(1), levels) - 1).astype(jnp.float32) * tick_length
    state = jnp.concatenate([positions, velocities, accelerations, jerks], axis=0)
    for step in range(active_rows.shape[0]):
        now = (step + 1) * tick_length
        pred_pos, pred_vel = predict(state[0:3], state[3:6], state[6:9], state[9:12], now - last_time)
        rows = active_rows[step]
        targets = jnp.concatenate(
            [pred_pos[:, rows], pred_vel[:, rows], jnp.zeros((2, slot_cap), jnp.float32)], axis=0
        ).T
        row_counts = counts[step].reshape(n_grp, n_dev)[g_idx, :]
        packed = targets.reshape(slot_cap * 8 // LANES, LANES)
        copies = lax.optimization_barrier(jnp.broadcast_to(packed[None], (n_dev,) + packed.shape))
        row_targets = lax.all_to_all(copies, "dev", 0, 0, tiled=True).reshape(row_cap, 8)
        mine = jnp.concatenate([pred_pos, pred_vel], axis=0)
        spread = lax.optimization_barrier(jnp.broadcast_to(mine[None], (n_grp,) + mine.shape))
        src = lax.all_to_all(spread, "grp", 0, 0, tiled=True)
        src = src.transpose(1, 0, 2).reshape(6, n_grp * star_dev)
        partial = pair_terms(row_counts, row_targets, src, mass, soft_sq)
        received = lax.all_to_all(partial, "dev", 0, 0, tiled=True)
        own = jnp.sum(received, axis=0)[:6]
        own_count = row_counts[d_idx]
        span = now - last_time[rows]
        old = state[:, rows]
        new_pos, new_vel = correct(old[0:3], old[3:6], old[6:9], old[9:12], own[:3], own[3:], span)
        live = jnp.arange(slot_cap, dtype=jnp.int32) < own_count
        target = jnp.where(live, rows, star_dev)
        state = state.at[:, target].set(jnp.concatenate([new_pos, new_vel, own], axis=0), mode="drop")
        last_time = last_time.at[target].set(now, mode="drop")
    return (state[0:3], state[3:6], state[6:9], state[9:12])


def solution(mesh):
    placed = (
        P(None, ("grp", "dev")),
        P(None, ("grp", "dev")),
        P(None, ("grp", "dev")),
        P(None, ("grp", "dev")),
        P(("grp", "dev")),
        P(),
        P(None, ("grp", "dev")),
    )
    return jax.shard_map(
        shards,
        mesh=mesh,
        in_specs=placed,
        out_specs=(
            P(None, ("grp", "dev")),
            P(None, ("grp", "dev")),
            P(None, ("grp", "dev")),
            P(None, ("grp", "dev")),
        ),
        check_vma=False,
    )
```

```python
import math

import jax
import jax.numpy as jnp
from jax import lax
from jax.experimental import pallas as pl
from jax.experimental.pallas import tpu as pltpu
from jax.sharding import PartitionSpec as P

tick_length = 1.0 / 128.0


LANES = 128
SUB = 8


def _pair_terms_kernel(cnt_ref, raw_ref, src_ref, out_ref, acc_ref, tgt_ref, *, soft_sq, mass, n_chunks, n_owner, slot_cap):
    acc_ref[...] = jnp.zeros(acc_ref.shape, jnp.float32)

    def unflip(o, carry):
        wide = jnp.concatenate([raw_ref[o], jnp.zeros((LANES - 8, slot_cap), jnp.float32)], axis=0)
        tgt_ref[pl.ds(pl.multiple_of(o * slot_cap, slot_cap), slot_cap), :] = wide.T
        return carry

    lax.fori_loop(0, n_owner, unflip, 0)

    def one_group(base, n_half):
        tile = tgt_ref[pl.ds(base, n_half * SUB), :]
        halves = []
        for h in range(n_half):
            part = tile[h * SUB:(h + 1) * SUB, :]
            halves.append([jnp.broadcast_to(part[:, k:k + 1], (SUB, LANES)) for k in range(6)])

        def chunk(c, accs):
            off = pl.multiple_of(c * LANES, LANES)
            s = [src_ref[k, :, pl.ds(off, LANES)] for k in range(6)]
            new = []
            for h in range(n_half):
                t = halves[h]
                a = accs[6 * h:6 * h + 6]
                dx = s[0] - t[0]
                dy = s[1] - t[1]
                dz = s[2] - t[2]
                ux = s[3] - t[3]
                uy = s[4] - t[4]
                uz = s[5] - t[5]
                r2 = dx * dx + dy * dy + dz * dz + soft_sq
                inv = lax.rsqrt(r2)
                inv2 = inv * inv
                w = inv * inv2
                al = 3.0 * (dx * ux + dy * uy + dz * uz) * inv2
                new += [
                    a[0] + w * dx,
                    a[1] + w * dy,
                    a[2] + w * dz,
                    a[3] + w * (ux - al * dx),
                    a[4] + w * (uy - al * dy),
                    a[5] + w * (uz - al * dz),
                ]
            return tuple(new)

        zero = jnp.zeros((SUB, LANES), jnp.float32)
        accs = lax.fori_loop(0, n_chunks, chunk, (zero,) * (6 * n_half), unroll=16)
        for h in range(n_half):
            for k in range(6):
                total = jnp.sum(accs[6 * h + k], axis=1, keepdims=True) * mass
                acc_ref[pl.ds(base + h * SUB, SUB), pl.ds(k, 1)] = total

    def one_owner(o, carry):
        count = jnp.clip(cnt_ref[o], 0, slot_cap)
        n_full = count // (2 * SUB)
        rest = count - n_full * (2 * SUB)
        tail = pl.multiple_of(o * slot_cap + n_full * (2 * SUB), SUB)

        def body(gi, c):
            one_group(pl.multiple_of(o * slot_cap + gi * (2 * SUB), 2 * SUB), 2)
            return c

        lax.fori_loop(0, n_full, body, 0)

        @pl.when(rest > SUB)
        def _():
            one_group(tail, 2)

        @pl.when((rest > 0) & (rest <= SUB))
        def _():
            one_group(tail, 1)

        return carry

    lax.fori_loop(0, n_owner, one_owner, 0)

    def flip(o, carry):
        block = acc_ref[pl.ds(pl.multiple_of(o * slot_cap, slot_cap), slot_cap), :]
        out_ref[o] = block.T[:8, :]
        return carry

    lax.fori_loop(0, n_owner, flip, 0)


def pair_terms(col_counts, tgt, src, mass, soft_sq, interpret=False):
    n_owner = tgt.shape[0]
    cap = n_owner * tgt.shape[2]
    n_src = src.shape[1]
    src_b = jnp.broadcast_to(src[:, None, :], (6, SUB, n_src))
    kernel = lambda *refs: _pair_terms_kernel(
        *refs, soft_sq=soft_sq, mass=mass, n_chunks=n_src // LANES, n_owner=n_owner, slot_cap=cap // n_owner
    )
    return pl.pallas_call(
        kernel,
        out_shape=jax.ShapeDtypeStruct((n_owner, 8, cap // n_owner), jnp.float32),
        in_specs=[
            pl.BlockSpec(memory_space=pltpu.SMEM),
            pl.BlockSpec(memory_space=pltpu.VMEM),
            pl.BlockSpec(memory_space=pltpu.VMEM),
        ],
        out_specs=pl.BlockSpec(memory_space=pltpu.VMEM),
        scratch_shapes=[pltpu.VMEM((cap, LANES), jnp.float32), pltpu.VMEM((cap, LANES), jnp.float32)],
        interpret=interpret,
    )(col_counts.astype(jnp.int32), tgt, src_b)


def pair_block(targets, src_pos, src_vel, mass, soft_sq):
    gap_x = src_pos[0][None, :] - targets[0][:, None]
    gap_y = src_pos[1][None, :] - targets[1][:, None]
    gap_z = src_pos[2][None, :] - targets[2][:, None]
    drift_x = src_vel[0][None, :] - targets[3][:, None]
    drift_y = src_vel[1][None, :] - targets[4][:, None]
    drift_z = src_vel[2][None, :] - targets[5][:, None]
    squared = gap_x * gap_x + gap_y * gap_y + gap_z * gap_z + soft_sq
    inverse = lax.rsqrt(squared)
    weight = mass * inverse * inverse * inverse
    along = 3.0 * (gap_x * drift_x + gap_y * drift_y + gap_z * drift_z) * inverse * inverse
    return jnp.stack(
        [
            jnp.sum(weight * gap_x, axis=1),
            jnp.sum(weight * gap_y, axis=1),
            jnp.sum(weight * gap_z, axis=1),
            jnp.sum(weight * (drift_x - along * gap_x), axis=1),
            jnp.sum(weight * (drift_y - along * gap_y), axis=1),
            jnp.sum(weight * (drift_z - along * gap_z), axis=1),
        ]
    )


def block_terms(packed, src_pos, src_vel, mass, soft_sq):
    width, total = packed.shape
    block = math.gcd(total, 2048)
    grouped = packed.reshape(width, total // block, block).transpose(1, 0, 2)
    result = lax.map(lambda targets: pair_block(targets, src_pos, src_vel, mass, soft_sq), grouped)
    return result.transpose(1, 0, 2).reshape(width, total)


def predict(positions, velocities, accelerations, jerks, elapsed):
    span = elapsed[None, :]
    pred_pos = (
        positions
        + span * velocities
        + 0.5 * span * span * accelerations
        + span * span * span / 6.0 * jerks
    )
    pred_vel = velocities + span * accelerations + 0.5 * span * span * jerks
    return (pred_pos, pred_vel)


def correct(old_pos, old_vel, old_acc, old_jerk, force, jerk_new, span):
    span = span[None, :]
    new_vel = old_vel + 0.5 * span * (old_acc + force) + span * span / 12.0 * (old_jerk - jerk_new)
    new_pos = old_pos + 0.5 * span * (old_vel + new_vel) + span * span / 12.0 * (old_acc - force)
    return (new_pos, new_vel)


def shards(positions, velocities, accelerations, jerks, levels, counts, active_rows):
    n_grp = lax.axis_size("grp")
    n_dev = lax.axis_size("dev")
    g_idx = lax.axis_index("grp")
    d_idx = lax.axis_index("dev")
    devices_all = n_grp * n_dev
    star_dev = positions.shape[1]
    slot_cap = active_rows.shape[1]
    stars_all = star_dev * devices_all
    mass = 1.0 / stars_all
    soft_sq = 0.0004 * (131072.0 / stars_all) ** (2.0 / 3.0)
    row_cap = n_dev * slot_cap
    last_time = -(jnp.left_shift(jnp.int32(1), levels) - 1).astype(jnp.float32) * tick_length
    state = jnp.concatenate([positions, velocities, accelerations, jerks], axis=0)
    for step in range(active_rows.shape[0]):
        now = (step + 1) * tick_length
        pred_pos, pred_vel = predict(state[0:3], state[3:6], state[6:9], state[9:12], now - last_time)
        rows = active_rows[step]
        targets = jnp.concatenate(
            [pred_pos[:, rows], pred_vel[:, rows], jnp.zeros((2, slot_cap), jnp.float32)], axis=0
        )
        row_counts = counts[step].reshape(n_grp, n_dev)[g_idx, :]
        copies = lax.optimization_barrier(jnp.broadcast_to(targets[None], (n_dev,) + targets.shape))
        row_targets = lax.all_to_all(copies, "dev", 0, 0, tiled=True)
        mine = jnp.concatenate([pred_pos, pred_vel], axis=0)
        spread = lax.optimization_barrier(jnp.broadcast_to(mine[None], (n_grp,) + mine.shape))
        src = lax.all_to_all(spread, "grp", 0, 0, tiled=True)
        src = src.transpose(1, 0, 2).reshape(6, n_grp * star_dev)
        partial = pair_terms(row_counts, row_targets, src, mass, soft_sq)
        received = lax.all_to_all(partial, "dev", 0, 0, tiled=True)
        own = jnp.sum(received, axis=0)[:6]
        own_count = row_counts[d_idx]
        span = now - last_time[rows]
        old = state[:, rows]
        new_pos, new_vel = correct(old[0:3], old[3:6], old[6:9], old[9:12], own[:3], own[3:], span)
        live = jnp.arange(slot_cap, dtype=jnp.int32) < own_count
        target = jnp.where(live, rows, star_dev)
        state = state.at[:, target].set(jnp.concatenate([new_pos, new_vel, own], axis=0), mode="drop")
        last_time = last_time.at[target].set(now, mode="drop")
    return (state[0:3], state[3:6], state[6:9], state[9:12])


def solution(mesh):
    placed = (
        P(None, ("grp", "dev")),
        P(None, ("grp", "dev")),
        P(None, ("grp", "dev")),
        P(None, ("grp", "dev")),
        P(("grp", "dev")),
        P(),
        P(None, ("grp", "dev")),
    )
    return jax.shard_map(
        shards,
        mesh=mesh,
        in_specs=placed,
        out_specs=(
            P(None, ("grp", "dev")),
            P(None, ("grp", "dev")),
            P(None, ("grp", "dev")),
            P(None, ("grp", "dev")),
        ),
        check_vma=False,
    )
```

```python
import math

import jax
import jax.numpy as jnp
from jax import lax
from jax.experimental import pallas as pl
from jax.experimental.pallas import tpu as pltpu
from jax.sharding import PartitionSpec as P

tick_length = 1.0 / 128.0


LANES = 128
SUB = 8


def _pair_terms_kernel(cnt_ref, tgt_ref, src_ref, out_ref, acc_ref, *, soft_sq, mass, n_chunks, n_owner, slot_cap):
    acc_ref[...] = jnp.zeros(acc_ref.shape, jnp.float32)

    def one_group(base, n_half):
        tile = tgt_ref[pl.ds(base, n_half * SUB), :]
        halves = []
        for h in range(n_half):
            part = tile[h * SUB:(h + 1) * SUB, :]
            halves.append([jnp.broadcast_to(part[:, k:k + 1], (SUB, LANES)) for k in range(6)])

        def chunk(c, accs):
            off = pl.multiple_of(c * LANES, LANES)
            s = [src_ref[k, :, pl.ds(off, LANES)] for k in range(6)]
            new = []
            for h in range(n_half):
                t = halves[h]
                a = accs[6 * h:6 * h + 6]
                dx = s[0] - t[0]
                dy = s[1] - t[1]
                dz = s[2] - t[2]
                ux = s[3] - t[3]
                uy = s[4] - t[4]
                uz = s[5] - t[5]
                r2 = dx * dx + dy * dy + dz * dz + soft_sq
                inv = lax.rsqrt(r2)
                inv2 = inv * inv
                w = inv * inv2
                al = 3.0 * (dx * ux + dy * uy + dz * uz) * inv2
                new += [
                    a[0] + w * dx,
                    a[1] + w * dy,
                    a[2] + w * dz,
                    a[3] + w * (ux - al * dx),
                    a[4] + w * (uy - al * dy),
                    a[5] + w * (uz - al * dz),
                ]
            return tuple(new)

        zero = jnp.zeros((SUB, LANES), jnp.float32)
        accs = lax.fori_loop(0, n_chunks, chunk, (zero,) * (6 * n_half), unroll=16)
        for h in range(n_half):
            for k in range(6):
                total = jnp.sum(accs[6 * h + k], axis=1, keepdims=True) * mass
                acc_ref[pl.ds(base + h * SUB, SUB), pl.ds(k, 1)] = total

    def one_owner(o, carry):
        count = jnp.clip(cnt_ref[o], 0, slot_cap)
        n_full = count // (2 * SUB)
        rest = count - n_full * (2 * SUB)
        tail = pl.multiple_of(o * slot_cap + n_full * (2 * SUB), SUB)

        def body(gi, c):
            one_group(pl.multiple_of(o * slot_cap + gi * (2 * SUB), 2 * SUB), 2)
            return c

        lax.fori_loop(0, n_full, body, 0)

        @pl.when(rest > SUB)
        def _():
            one_group(tail, 2)

        @pl.when((rest > 0) & (rest <= SUB))
        def _():
            one_group(tail, 1)

        return carry

    lax.fori_loop(0, n_owner, one_owner, 0)

    def flip(o, carry):
        block = acc_ref[pl.ds(pl.multiple_of(o * slot_cap, slot_cap), slot_cap), :]
        out_ref[o] = block.T[:8, :]
        return carry

    lax.fori_loop(0, n_owner, flip, 0)


def pair_terms(col_counts, tgt, src, mass, soft_sq, interpret=False):
    cap = tgt.shape[0]
    n_owner = col_counts.shape[0]
    n_src = src.shape[1]
    src_b = jnp.broadcast_to(src[:, None, :], (6, SUB, n_src))
    kernel = lambda *refs: _pair_terms_kernel(
        *refs, soft_sq=soft_sq, mass=mass, n_chunks=n_src // LANES, n_owner=n_owner, slot_cap=cap // n_owner
    )
    return pl.pallas_call(
        kernel,
        out_shape=jax.ShapeDtypeStruct((n_owner, 8, cap // n_owner), jnp.float32),
        in_specs=[
            pl.BlockSpec(memory_space=pltpu.SMEM),
            pl.BlockSpec(memory_space=pltpu.VMEM),
            pl.BlockSpec(memory_space=pltpu.VMEM),
        ],
        out_specs=pl.BlockSpec(memory_space=pltpu.VMEM),
        scratch_shapes=[pltpu.VMEM((cap, LANES), jnp.float32)],
        interpret=interpret,
    )(col_counts.astype(jnp.int32), tgt, src_b)


def pair_block(targets, src_pos, src_vel, mass, soft_sq):
    gap_x = src_pos[0][None, :] - targets[0][:, None]
    gap_y = src_pos[1][None, :] - targets[1][:, None]
    gap_z = src_pos[2][None, :] - targets[2][:, None]
    drift_x = src_vel[0][None, :] - targets[3][:, None]
    drift_y = src_vel[1][None, :] - targets[4][:, None]
    drift_z = src_vel[2][None, :] - targets[5][:, None]
    squared = gap_x * gap_x + gap_y * gap_y + gap_z * gap_z + soft_sq
    inverse = lax.rsqrt(squared)
    weight = mass * inverse * inverse * inverse
    along = 3.0 * (gap_x * drift_x + gap_y * drift_y + gap_z * drift_z) * inverse * inverse
    return jnp.stack(
        [
            jnp.sum(weight * gap_x, axis=1),
            jnp.sum(weight * gap_y, axis=1),
            jnp.sum(weight * gap_z, axis=1),
            jnp.sum(weight * (drift_x - along * gap_x), axis=1),
            jnp.sum(weight * (drift_y - along * gap_y), axis=1),
            jnp.sum(weight * (drift_z - along * gap_z), axis=1),
        ]
    )


def block_terms(packed, src_pos, src_vel, mass, soft_sq):
    width, total = packed.shape
    block = math.gcd(total, 2048)
    grouped = packed.reshape(width, total // block, block).transpose(1, 0, 2)
    result = lax.map(lambda targets: pair_block(targets, src_pos, src_vel, mass, soft_sq), grouped)
    return result.transpose(1, 0, 2).reshape(width, total)


def predict(positions, velocities, accelerations, jerks, elapsed):
    span = elapsed[None, :]
    pred_pos = (
        positions
        + span * velocities
        + 0.5 * span * span * accelerations
        + span * span * span / 6.0 * jerks
    )
    pred_vel = velocities + span * accelerations + 0.5 * span * span * jerks
    return (pred_pos, pred_vel)


def correct(old_pos, old_vel, old_acc, old_jerk, force, jerk_new, span):
    span = span[None, :]
    new_vel = old_vel + 0.5 * span * (old_acc + force) + span * span / 12.0 * (old_jerk - jerk_new)
    new_pos = old_pos + 0.5 * span * (old_vel + new_vel) + span * span / 12.0 * (old_acc - force)
    return (new_pos, new_vel)


def shards(positions, velocities, accelerations, jerks, levels, counts, active_rows):
    n_grp = lax.axis_size("grp")
    n_dev = lax.axis_size("dev")
    g_idx = lax.axis_index("grp")
    d_idx = lax.axis_index("dev")
    devices_all = n_grp * n_dev
    star_dev = positions.shape[1]
    slot_cap = active_rows.shape[1]
    stars_all = star_dev * devices_all
    mass = 1.0 / stars_all
    soft_sq = 0.0004 * (131072.0 / stars_all) ** (2.0 / 3.0)
    row_cap = n_dev * slot_cap
    last_time = -(jnp.left_shift(jnp.int32(1), levels) - 1).astype(jnp.float32) * tick_length
    state = jnp.concatenate([positions, velocities, accelerations, jerks], axis=0)
    for step in range(active_rows.shape[0]):
        now = (step + 1) * tick_length
        pred_pos, pred_vel = predict(state[0:3], state[3:6], state[6:9], state[9:12], now - last_time)
        rows = active_rows[step]
        targets = jnp.concatenate(
            [pred_pos[:, rows], pred_vel[:, rows], jnp.zeros((2, slot_cap), jnp.float32)], axis=0
        ).T
        row_counts = counts[step].reshape(n_grp, n_dev)[g_idx, :]
        packed = targets.reshape(slot_cap * 8 // LANES, LANES)
        copies = jnp.broadcast_to(packed[None], (n_dev,) + packed.shape)
        row_targets = lax.all_to_all(copies, "dev", 0, 0, tiled=True).reshape(row_cap, 8)
        mine = jnp.concatenate([pred_pos, pred_vel], axis=0)
        spread = jnp.broadcast_to(mine[None], (n_grp,) + mine.shape)
        src = lax.all_to_all(spread, "grp", 0, 0, tiled=True)
        src = src.transpose(1, 0, 2).reshape(6, n_grp * star_dev)
        partial = pair_terms(row_counts, row_targets, src, mass, soft_sq)
        received = lax.all_to_all(partial, "dev", 0, 0, tiled=True)
        own = jnp.sum(received, axis=0)[:6]
        own_count = row_counts[d_idx]
        span = now - last_time[rows]
        old = state[:, rows]
        new_pos, new_vel = correct(old[0:3], old[3:6], old[6:9], old[9:12], own[:3], own[3:], span)
        live = jnp.arange(slot_cap, dtype=jnp.int32) < own_count
        target = jnp.where(live, rows, star_dev)
        state = state.at[:, target].set(jnp.concatenate([new_pos, new_vel, own], axis=0), mode="drop")
        last_time = last_time.at[target].set(now, mode="drop")
    return (state[0:3], state[3:6], state[6:9], state[9:12])


def solution(mesh):
    placed = (
        P(None, ("grp", "dev")),
        P(None, ("grp", "dev")),
        P(None, ("grp", "dev")),
        P(None, ("grp", "dev")),
        P(("grp", "dev")),
        P(),
        P(None, ("grp", "dev")),
    )
    return jax.shard_map(
        shards,
        mesh=mesh,
        in_specs=placed,
        out_specs=(
            P(None, ("grp", "dev")),
            P(None, ("grp", "dev")),
            P(None, ("grp", "dev")),
            P(None, ("grp", "dev")),
        ),
        check_vma=False,
    )
```

```python
import math

import jax
import jax.numpy as jnp
from jax import lax
from jax.experimental import pallas as pl
from jax.experimental.pallas import tpu as pltpu
from jax.sharding import PartitionSpec as P

tick_length = 1.0 / 128.0


LANES = 128
SUB = 8


def _pair_terms_kernel(cnt_ref, tgt_ref, raw_ref, out_ref, acc_ref, src_ref, *, soft_sq, mass, n_chunks, n_owner, slot_cap):
    acc_ref[...] = jnp.zeros(acc_ref.shape, jnp.float32)

    def spread(c, carry):
        off = pl.multiple_of(c * LANES, LANES)
        for k in range(6):
            src_ref[k, :, pl.ds(off, LANES)] = jnp.broadcast_to(raw_ref[pl.ds(k, 1), pl.ds(off, LANES)], (SUB, LANES))
        return carry

    lax.fori_loop(0, n_chunks, spread, 0)

    def one_group(base, n_half):
        tile = tgt_ref[pl.ds(base, n_half * SUB), :]
        halves = []
        for h in range(n_half):
            part = tile[h * SUB:(h + 1) * SUB, :]
            halves.append([jnp.broadcast_to(part[:, k:k + 1], (SUB, LANES)) for k in range(6)])

        def chunk(c, accs):
            off = pl.multiple_of(c * LANES, LANES)
            s = [src_ref[k, :, pl.ds(off, LANES)] for k in range(6)]
            new = []
            for h in range(n_half):
                t = halves[h]
                a = accs[6 * h:6 * h + 6]
                dx = s[0] - t[0]
                dy = s[1] - t[1]
                dz = s[2] - t[2]
                ux = s[3] - t[3]
                uy = s[4] - t[4]
                uz = s[5] - t[5]
                r2 = dx * dx + dy * dy + dz * dz + soft_sq
                inv = lax.rsqrt(r2)
                inv2 = inv * inv
                w = inv * inv2
                al = 3.0 * (dx * ux + dy * uy + dz * uz) * inv2
                new += [
                    a[0] + w * dx,
                    a[1] + w * dy,
                    a[2] + w * dz,
                    a[3] + w * (ux - al * dx),
                    a[4] + w * (uy - al * dy),
                    a[5] + w * (uz - al * dz),
                ]
            return tuple(new)

        zero = jnp.zeros((SUB, LANES), jnp.float32)
        accs = lax.fori_loop(0, n_chunks, chunk, (zero,) * (6 * n_half), unroll=16)
        for h in range(n_half):
            for k in range(6):
                total = jnp.sum(accs[6 * h + k], axis=1, keepdims=True) * mass
                acc_ref[pl.ds(base + h * SUB, SUB), pl.ds(k, 1)] = total

    def one_owner(o, carry):
        count = jnp.clip(cnt_ref[o], 0, slot_cap)
        n_full = count // (2 * SUB)
        rest = count - n_full * (2 * SUB)
        tail = pl.multiple_of(o * slot_cap + n_full * (2 * SUB), SUB)

        def body(gi, c):
            one_group(pl.multiple_of(o * slot_cap + gi * (2 * SUB), 2 * SUB), 2)
            return c

        lax.fori_loop(0, n_full, body, 0)

        @pl.when(rest > SUB)
        def _():
            one_group(tail, 2)

        @pl.when((rest > 0) & (rest <= SUB))
        def _():
            one_group(tail, 1)

        return carry

    lax.fori_loop(0, n_owner, one_owner, 0)

    def flip(o, carry):
        block = acc_ref[pl.ds(pl.multiple_of(o * slot_cap, slot_cap), slot_cap), :]
        out_ref[o] = block.T[:8, :]
        return carry

    lax.fori_loop(0, n_owner, flip, 0)


def pair_terms(col_counts, tgt, src, mass, soft_sq, interpret=False):
    cap = tgt.shape[0]
    n_owner = col_counts.shape[0]
    n_src = src.shape[1]
    kernel = lambda *refs: _pair_terms_kernel(
        *refs, soft_sq=soft_sq, mass=mass, n_chunks=n_src // LANES, n_owner=n_owner, slot_cap=cap // n_owner
    )
    return pl.pallas_call(
        kernel,
        out_shape=jax.ShapeDtypeStruct((n_owner, 8, cap // n_owner), jnp.float32),
        in_specs=[
            pl.BlockSpec(memory_space=pltpu.SMEM),
            pl.BlockSpec(memory_space=pltpu.VMEM),
            pl.BlockSpec(memory_space=pltpu.VMEM),
        ],
        out_specs=pl.BlockSpec(memory_space=pltpu.VMEM),
        scratch_shapes=[pltpu.VMEM((cap, LANES), jnp.float32), pltpu.VMEM((6, SUB, n_src), jnp.float32)],
        interpret=interpret,
    )(col_counts.astype(jnp.int32), tgt, src)


def pair_block(targets, src_pos, src_vel, mass, soft_sq):
    gap_x = src_pos[0][None, :] - targets[0][:, None]
    gap_y = src_pos[1][None, :] - targets[1][:, None]
    gap_z = src_pos[2][None, :] - targets[2][:, None]
    drift_x = src_vel[0][None, :] - targets[3][:, None]
    drift_y = src_vel[1][None, :] - targets[4][:, None]
    drift_z = src_vel[2][None, :] - targets[5][:, None]
    squared = gap_x * gap_x + gap_y * gap_y + gap_z * gap_z + soft_sq
    inverse = lax.rsqrt(squared)
    weight = mass * inverse * inverse * inverse
    along = 3.0 * (gap_x * drift_x + gap_y * drift_y + gap_z * drift_z) * inverse * inverse
    return jnp.stack(
        [
            jnp.sum(weight * gap_x, axis=1),
            jnp.sum(weight * gap_y, axis=1),
            jnp.sum(weight * gap_z, axis=1),
            jnp.sum(weight * (drift_x - along * gap_x), axis=1),
            jnp.sum(weight * (drift_y - along * gap_y), axis=1),
            jnp.sum(weight * (drift_z - along * gap_z), axis=1),
        ]
    )


def block_terms(packed, src_pos, src_vel, mass, soft_sq):
    width, total = packed.shape
    block = math.gcd(total, 2048)
    grouped = packed.reshape(width, total // block, block).transpose(1, 0, 2)
    result = lax.map(lambda targets: pair_block(targets, src_pos, src_vel, mass, soft_sq), grouped)
    return result.transpose(1, 0, 2).reshape(width, total)


def predict(positions, velocities, accelerations, jerks, elapsed):
    span = elapsed[None, :]
    pred_pos = (
        positions
        + span * velocities
        + 0.5 * span * span * accelerations
        + span * span * span / 6.0 * jerks
    )
    pred_vel = velocities + span * accelerations + 0.5 * span * span * jerks
    return (pred_pos, pred_vel)


def correct(old_pos, old_vel, old_acc, old_jerk, force, jerk_new, span):
    span = span[None, :]
    new_vel = old_vel + 0.5 * span * (old_acc + force) + span * span / 12.0 * (old_jerk - jerk_new)
    new_pos = old_pos + 0.5 * span * (old_vel + new_vel) + span * span / 12.0 * (old_acc - force)
    return (new_pos, new_vel)


def shards(positions, velocities, accelerations, jerks, levels, counts, active_rows):
    n_grp = lax.axis_size("grp")
    n_dev = lax.axis_size("dev")
    g_idx = lax.axis_index("grp")
    d_idx = lax.axis_index("dev")
    devices_all = n_grp * n_dev
    star_dev = positions.shape[1]
    slot_cap = active_rows.shape[1]
    stars_all = star_dev * devices_all
    mass = 1.0 / stars_all
    soft_sq = 0.0004 * (131072.0 / stars_all) ** (2.0 / 3.0)
    row_cap = n_dev * slot_cap
    last_time = -(jnp.left_shift(jnp.int32(1), levels) - 1).astype(jnp.float32) * tick_length
    state = jnp.concatenate([positions, velocities, accelerations, jerks], axis=0)
    for step in range(active_rows.shape[0]):
        now = (step + 1) * tick_length
        pred_pos, pred_vel = predict(state[0:3], state[3:6], state[6:9], state[9:12], now - last_time)
        rows = active_rows[step]
        targets = jnp.concatenate(
            [pred_pos[:, rows], pred_vel[:, rows], jnp.zeros((2, slot_cap), jnp.float32)], axis=0
        ).T
        row_counts = counts[step].reshape(n_grp, n_dev)[g_idx, :]
        packed = targets.reshape(slot_cap * 8 // LANES, LANES)
        copies = lax.optimization_barrier(jnp.broadcast_to(packed[None], (n_dev,) + packed.shape))
        row_targets = lax.all_to_all(copies, "dev", 0, 0, tiled=True).reshape(row_cap, 8)
        mine = jnp.concatenate([pred_pos, pred_vel], axis=0)
        spread = lax.optimization_barrier(jnp.broadcast_to(mine[None], (n_grp,) + mine.shape))
        src = lax.all_to_all(spread, "grp", 0, 0, tiled=True)
        src = src.transpose(1, 0, 2).reshape(6, n_grp * star_dev)
        partial = pair_terms(row_counts, row_targets, src, mass, soft_sq)
        received = lax.all_to_all(partial, "dev", 0, 0, tiled=True)
        own = jnp.sum(received, axis=0)[:6]
        own_count = row_counts[d_idx]
        span = now - last_time[rows]
        old = state[:, rows]
        new_pos, new_vel = correct(old[0:3], old[3:6], old[6:9], old[9:12], own[:3], own[3:], span)
        live = jnp.arange(slot_cap, dtype=jnp.int32) < own_count
        target = jnp.where(live, rows, star_dev)
        state = state.at[:, target].set(jnp.concatenate([new_pos, new_vel, own], axis=0), mode="drop")
        last_time = last_time.at[target].set(now, mode="drop")
    return (state[0:3], state[3:6], state[6:9], state[9:12])


def solution(mesh):
    placed = (
        P(None, ("grp", "dev")),
        P(None, ("grp", "dev")),
        P(None, ("grp", "dev")),
        P(None, ("grp", "dev")),
        P(("grp", "dev")),
        P(),
        P(None, ("grp", "dev")),
    )
    return jax.shard_map(
        shards,
        mesh=mesh,
        in_specs=placed,
        out_specs=(
            P(None, ("grp", "dev")),
            P(None, ("grp", "dev")),
            P(None, ("grp", "dev")),
            P(None, ("grp", "dev")),
        ),
        check_vma=False,
    )
```
